32 devices in a mesh: pipe: 4 (over x, core), seq: 8 (over z, y).
Axes of the slice: x: 2, y: 2, z: 4, core: 2. Of those that a mesh axis runs over, the one named last changes fastest.
Arguments:
- queries: bfloat16 [4, 1024, 4096], P('pipe', 'seq'), may hold values from -6 to 6
- key_heads: bfloat16 [4, 1024, 512], P('pipe', 'seq'), may hold values from -6 to 6
- inputs: bfloat16 [4, 1024, 4096], P('pipe', 'seq'), may hold values from -6 to 6
- cotangent: bfloat16 [1024, 4096], P('seq'), may hold values from -6 to 6
- lengths: int32 [8], replicated, may hold values from 1 to 128, 768 in all
Outputs:
- grad_queries: bfloat16 [4, 1024, 4096], P('pipe', 'seq')
- grad_keys: bfloat16 [4, 1024, 512], P('pipe', 'seq')
- grad_inputs: bfloat16 [4, 1024, 4096], P('pipe', 'seq')
The draws below stay inside these ranges and needn't reach their ends.
Inputs may be any that keep to these rules, and one draw needn't show every extreme that they name: lengths sum to 768 and one of them equals 128.
All inputs are finite; a program needn't handle non-finite values.
Results may differ from the reference program's by a relative error of at most 0.013.
Values may be sent and summed in bfloat16 or wider, within the bound.
No kernel may reach another device: no remote copies, remote signals or barrier semaphores. Data moves between devices by JAX's collectives and lax.ppermute only.
A program may use at most 64 MiB of HBM per device.

```python
import math
import jax
import jax.numpy as jnp
import numpy as np
from jax import lax

H = 32
KVH = 4
DH = 128
BLK = 128
LAYERS = 4
SEQLEN = 1024
NBLK = 8
N_SEQ = 8


def draw_queries(key, part):
    shape = (LAYERS, SEQLEN, H, DH)
    entries = jnp.clip(jax.random.normal(jax.random.fold_in(key, 1), shape, jnp.float32), -6.0, 6.0)
    return entries.reshape(LAYERS, SEQLEN, H * DH).astype(jnp.bfloat16)


def draw_key_heads(key, part):
    shape = (LAYERS, SEQLEN, KVH, DH)
    entries = jnp.clip(jax.random.normal(jax.random.fold_in(key, 2), shape, jnp.float32), -6.0, 6.0)
    return entries.reshape(LAYERS, SEQLEN, KVH * DH).astype(jnp.bfloat16)


def block_levels(rng, extent, shards, least, high):
    def one(axis_at, parts):
        draws = jax.random.uniform(jax.random.fold_in(jax.random.fold_in(rng, 6), axis_at), (parts,), jnp.float32, least / len(shards), high / len(shards))
        return jnp.repeat(jnp.exp(draws), extent[axis_at] // parts).reshape((-1,) + (1,) * (len(extent) - axis_at - 1))

    factor_of = one(*shards[0])
    for cut in shards[1:]:
        factor_of = factor_of * one(*cut)
    return factor_of


def length_profile(number_of, total, reach, skew):
    portions = [(1 << 20) // math.isqrt(rank ** skew) + 1 for rank in range(2, number_of + 1)]
    surplus, given = total - reach - (number_of - 1), [1] * (number_of - 1)
    while surplus > 0:
        candidates = [i for i in range(number_of - 1) if given[i] < reach]
        whole, remaining = sum([portions[i] for i in candidates]), surplus
        for i in candidates:
            extra = min(reach - given[i], max(1, remaining * portions[i] // whole), surplus)
            given[i] = given[i] + extra
            surplus = surplus - extra
    return np.array([reach] + given)


def uneven(rng, number_of, total, limit, skew):
    if number_of == 2:
        one = jax.random.randint(rng, (), max(1, total - limit), min(limit, total - 1) + 1)
        return jnp.stack([one, total - one])
    sizes = jnp.asarray(length_profile(number_of, total, limit, skew), jnp.int32)
    twos = (number_of - 1) // 2
    source_of, receiver = sizes[1:1 + 2 * twos:2], sizes[2:2 + 2 * twos:2]
    room = jnp.minimum(source_of - 1, limit - receiver)
    moved = jax.random.randint(jax.random.fold_in(rng, 1), (twos,), 0, 1 << 20) % (room + 1)
    sizes = sizes.at[1:1 + 2 * twos:2].set(source_of - moved).at[2:2 + 2 * twos:2].set(receiver + moved)
    return sizes[jax.random.permutation(jax.random.fold_in(rng, 2), number_of)]


def noise(stream_key, extent, deviation, bound, split=(), kind=jnp.bfloat16):
    values = deviation * jax.random.normal(stream_key, extent, jnp.float32)
    if split:
        values = values * block_levels(stream_key, extent, split, -0.22, 0.18)
    return jnp.clip(values, -bound, bound).astype(kind)


def setup_inputs(seed: int = 0) -> dict:
    splits = jax.random.split(jax.random.key(seed), 6)
    return {
        "queries": draw_queries(jax.random.fold_in(splits[5], 71), 0),
        "key_heads": draw_key_heads(jax.random.fold_in(splits[5], 71), 0),
        "inputs": noise(splits[2], (LAYERS, SEQLEN, H * DH), 1.0, 6.0, ((0, 4), (1, 8))),
        "cotangent": noise(splits[3], (SEQLEN, H * DH), 1.0, 6.0, ((0, 8),)),
        "lengths": uneven(splits[4], NBLK, 3 * BLK * NBLK // 4, BLK, 0).astype(jnp.int32),
    }


def key_pair(block_rows):
    first_block = jnp.broadcast_to(block_rows[:1], block_rows.shape)
    return jnp.concatenate([first_block, block_rows], axis=1)

def visible(lengths, block_count, block_len):
    shape = (block_count, block_len, 2 * block_len)
    row_index = lax.broadcasted_iota(jnp.int32, shape, 1)
    col_index = lax.broadcasted_iota(jnp.int32, shape, 2)
    block_index = lax.broadcasted_iota(jnp.int32, shape, 0)
    in_first = col_index < block_len
    offset = jnp.where(in_first, col_index, col_index - block_len)
    own_len = lengths.astype(jnp.int32)[:, None, None]
    first_ok = in_first & (offset < lengths[0]) & ((block_index > 0) | (offset <= row_index))
    own_ok = jnp.logical_not(in_first) & (block_index > 0) & (offset <= row_index) & (offset < own_len)
    return (first_ok | own_ok)[:, None]

def fold_keys(key_terms, block_len):
    own_part = key_terms[:, block_len:]
    first_part = lax.optimization_barrier(jnp.sum(key_terms[:, :block_len], axis=0))
    return own_part.at[0].add(first_part)

def fold_value(key_terms, block_len, groups):
    own_part = key_terms[:, block_len:]
    first_terms = key_terms[:, :block_len]
    grouped = first_terms.reshape((groups, first_terms.shape[0] // groups) + first_terms.shape[1:])
    partial_low = lax.optimization_barrier(lax.optimization_barrier(jnp.sum(grouped, axis=1)).astype(jnp.bfloat16))
    first_part = lax.optimization_barrier(jnp.sum(partial_low.astype(jnp.float32), axis=0))
    return own_part.at[0].add(first_part)

def probabilities(query_blocks, keys_both, allowed, score_scale):
    scores = jnp.einsum('bihd,bjhd->bhij', query_blocks.astype(jnp.float32), keys_both.astype(jnp.float32)) * score_scale
    scores = jnp.where(allowed, scores, -jnp.inf)
    row_max = lax.optimization_barrier(jnp.max(scores, axis=-1, keepdims=True))
    exp_scores = jnp.exp(scores - row_max)
    return exp_scores / lax.optimization_barrier(jnp.sum(exp_scores, axis=-1, keepdims=True))

def value_grad(probs_low, grad_blocks, block_len, groups):
    key_terms = jnp.einsum('bhij,bihd->bjhd', probs_low.astype(jnp.float32), grad_blocks.astype(jnp.float32))
    return (grad_blocks.astype(jnp.float32) + fold_value(key_terms, block_len, groups)).astype(jnp.bfloat16)

def weight_grads(softmax_probs, probs_low, query_blocks, keys_both, values_both, grad_blocks, score_scale, block_len):
    grad_wide = grad_blocks.astype(jnp.float32)
    output = jnp.einsum('bhij,bjhd->bihd', probs_low.astype(jnp.float32), values_both.astype(jnp.float32))
    row_dot = jnp.transpose(lax.optimization_barrier(jnp.sum(grad_wide * output, axis=-1)), (0, 2, 1))[..., None]
    grad_probs = jnp.einsum('bihd,bjhd->bhij', grad_wide, values_both.astype(jnp.float32))
    grad_scores = (softmax_probs * (grad_probs - row_dot)).astype(jnp.bfloat16)
    grad_query = (jnp.einsum('bhij,bjhd->bihd', grad_scores.astype(jnp.float32), keys_both.astype(jnp.float32)) * score_scale).astype(jnp.bfloat16)
    key_terms = jnp.einsum('bhij,bihd->bjhd', grad_scores.astype(jnp.float32), query_blocks.astype(jnp.float32))
    grad_key = (fold_keys(key_terms, block_len) * score_scale).astype(jnp.bfloat16)
    return (grad_query, grad_key)

def reference(queries, key_heads, inputs, cotangent, lengths):
    seq_len = queries.shape[1]
    block_count = seq_len // BLK
    group_size = H // KVH
    score_scale = DH ** (-0.5)
    allowed = visible(lengths, block_count, BLK)
    grad_rows = cotangent
    query_list = []
    key_list = []
    input_list = []
    for layer_index in range(LAYERS - 1, -1, -1):
        query_blocks = queries[layer_index].reshape(block_count, BLK, H, DH)
        spread_keys = jnp.broadcast_to(key_heads[layer_index].reshape(seq_len, KVH, 1, DH), (seq_len, KVH, group_size, DH))
        keys_both = key_pair(spread_keys.reshape(block_count, BLK, H, DH))
        values_both = key_pair(inputs[layer_index].reshape(block_count, BLK, H, DH))
        grad_blocks = grad_rows.reshape(block_count, BLK, H, DH)
        softmax_probs = probabilities(query_blocks, keys_both, allowed, score_scale)
        probs_low = softmax_probs.astype(jnp.bfloat16)
        new_grad = value_grad(probs_low, grad_blocks, BLK, N_SEQ)
        grad_query, grad_key = weight_grads(softmax_probs, probs_low, query_blocks, keys_both, values_both, grad_blocks, score_scale, BLK)
        key_sum = lax.optimization_barrier(jnp.sum(grad_key.reshape(seq_len, KVH, group_size, DH).astype(jnp.float32), axis=2))
        grad_rows = new_grad.reshape(seq_len, H * DH)
        query_list.insert(0, grad_query.reshape(seq_len, H * DH))
        key_list.insert(0, key_sum.astype(jnp.bfloat16).reshape(seq_len, KVH * DH))
        input_list.insert(0, grad_rows)
    return (jnp.stack(query_list), jnp.stack(key_list), jnp.stack(input_list))
```

```python
import jax
import jax.numpy as jnp
from jax import lax
from jax.sharding import PartitionSpec as P

DH = 128
BLK = 128


def from_behind(value, axis, steps):
    count = lax.axis_size(axis)
    leading, last = (max(0, -steps), min(count, count - steps))
    return lax.ppermute(value, axis, [(source, source + steps) for source in range(leading, last)])


def key_pair(block_rows):
    first_block = jnp.broadcast_to(block_rows[:1], block_rows.shape)
    return jnp.concatenate([first_block, block_rows], axis=1)


def visible(lengths, block_count, block_len):
    shape = (block_count, block_len, 2 * block_len)
    row_index = lax.broadcasted_iota(jnp.int32, shape, 1)
    col_index = lax.broadcasted_iota(jnp.int32, shape, 2)
    block_index = lax.broadcasted_iota(jnp.int32, shape, 0)
    in_first = col_index < block_len
    offset = jnp.where(in_first, col_index, col_index - block_len)
    own_len = lengths[:, None, None]
    first_ok = in_first & (offset < lengths[0]) & ((block_index > 0) | (offset <= row_index))
    own_ok = (
        jnp.logical_not(in_first) & (block_index > 0) & (offset <= row_index) & (offset < own_len)
    )
    return (first_ok | own_ok)[:, None]


def fold_keys(key_terms, block_len):
    own_part = key_terms[:, block_len:]
    first_part = jnp.sum(key_terms[:, :block_len], axis=0)
    return own_part.at[0].add(first_part)


def fold_value(key_terms, block_len, groups):
    own_part = key_terms[:, block_len:]
    first_terms = key_terms[:, :block_len]
    grouped = first_terms.reshape((groups, first_terms.shape[0] // groups) + first_terms.shape[1:])
    partial_low = lax.optimization_barrier(jnp.sum(grouped, axis=1).astype(jnp.bfloat16))
    first_part = jnp.sum(partial_low.astype(jnp.float32), axis=0)
    return own_part.at[0].add(first_part)


def probabilities(query_blocks, keys_both, allowed, score_scale):
    scores = (
        jnp.einsum("bihd,bjhd->bhij", query_blocks, keys_both, preferred_element_type=jnp.float32)
        * score_scale
    )
    scores = jnp.where(allowed, scores, -jnp.inf)
    row_max = jnp.max(scores, axis=-1, keepdims=True)
    exp_scores = jnp.exp(scores - row_max)
    return exp_scores / jnp.sum(exp_scores, axis=-1, keepdims=True)


def value_grad(probs_low, grad_blocks, block_len, groups):
    key_terms = jnp.einsum(
        "bhij,bihd->bjhd", probs_low, grad_blocks, preferred_element_type=jnp.float32
    )
    return (grad_blocks.astype(jnp.float32) + fold_value(key_terms, block_len, groups)).astype(
        jnp.bfloat16
    )


def score_grads(
    softmax_probs, probs_low, query_blocks, keys_both, values_both, grad_blocks, score_scale
):
    output = jnp.einsum(
        "bhij,bjhd->bihd", probs_low, values_both, preferred_element_type=jnp.float32
    )
    row_dot = jnp.transpose(jnp.sum(grad_blocks.astype(jnp.float32) * output, axis=-1), (0, 2, 1))[
        ..., None
    ]
    grad_probs = jnp.einsum(
        "bihd,bjhd->bhij", grad_blocks, values_both, preferred_element_type=jnp.float32
    )
    grad_scores = (softmax_probs * (grad_probs - row_dot)).astype(jnp.bfloat16)
    grad_query = (
        jnp.einsum("bhij,bjhd->bihd", grad_scores, keys_both, preferred_element_type=jnp.float32)
        * score_scale
    ).astype(jnp.bfloat16)
    key_terms = jnp.einsum(
        "bhij,bihd->bjhd", grad_scores, query_blocks, preferred_element_type=jnp.float32
    )
    return (grad_query, key_terms)


def weight_grads(
    softmax_probs,
    probs_low,
    query_blocks,
    keys_both,
    values_both,
    grad_blocks,
    score_scale,
    block_len,
):
    grad_query, key_terms = score_grads(
        softmax_probs, probs_low, query_blocks, keys_both, values_both, grad_blocks, score_scale
    )
    grad_key = (fold_keys(key_terms, block_len) * score_scale).astype(jnp.bfloat16)
    return (grad_query, grad_key)


def on_device(queries, key_heads, inputs, cotangent, lengths):
    section_count = lax.axis_size("pipe")
    section_index = lax.axis_index("pipe")
    seq_ways = lax.axis_size("seq")
    tok_rows = queries.shape[1]
    full_width = queries.shape[2]
    head_count = full_width // DH
    kv_count = key_heads.shape[2] // DH
    group_size = head_count // kv_count
    seq_len = tok_rows * seq_ways
    block_count = seq_len // BLK
    local_heads = head_count // seq_ways
    score_scale = DH ** (-0.5)
    last_section = section_count - 1
    live_tick = last_section - section_index

    def to_heads(flat_rows):
        return flat_rows.reshape(block_count, BLK, local_heads, DH)

    def to_flat(block_rows):
        return block_rows.reshape(seq_len, local_heads * DH)

    stacked = jnp.stack([queries[0], inputs[0], cotangent])
    stacked_heads = lax.all_to_all(stacked, "seq", split_axis=2, concat_axis=1, tiled=True)
    query_flat, input_flat, cot_flat = stacked_heads[0], stacked_heads[1], stacked_heads[2]
    kv_pick = (jnp.arange(seq_ways) * local_heads) // group_size
    key_rows = key_heads[0].reshape(tok_rows, kv_count, DH)[:, kv_pick, :]
    key_flat = lax.all_to_all(key_rows, "seq", split_axis=1, concat_axis=0, tiled=True)
    key_blocks = jnp.broadcast_to(
        key_flat.reshape(block_count, BLK, 1, DH), (block_count, BLK, local_heads, DH)
    )
    query_blocks = to_heads(query_flat)
    keys_both = key_pair(key_blocks)
    values_both = key_pair(to_heads(input_flat))
    allowed = visible(lengths, block_count, BLK)
    softmax_probs = probabilities(query_blocks, keys_both, allowed, score_scale)
    probs_low = softmax_probs.astype(jnp.bfloat16)

    arrived = jnp.zeros_like(cot_flat)
    held_in = cot_flat
    held_out = cot_flat
    for tick in range(section_count):
        sender = last_section - tick
        grad_in = jnp.where(section_index == last_section, cot_flat, arrived)
        new_grad = to_flat(value_grad(probs_low, to_heads(grad_in), BLK, seq_ways))
        active = tick == live_tick
        held_in = jnp.where(active, grad_in, held_in)
        held_out = jnp.where(active, new_grad, held_out)
        if sender > 0:
            arrived = lax.ppermute(new_grad, "pipe", [(sender, sender - 1)])

    grad_query, grad_key = weight_grads(
        softmax_probs,
        probs_low,
        query_blocks,
        keys_both,
        values_both,
        to_heads(held_in),
        score_scale,
        BLK,
    )
    pair_out = lax.all_to_all(
        jnp.stack([to_flat(grad_query), held_out]), "seq", split_axis=1, concat_axis=2, tiled=True
    )
    if local_heads == 1:
        key_part = grad_key.reshape(seq_len, DH)
    else:
        key_part = jnp.sum(grad_key.astype(jnp.float32), axis=2).reshape(seq_len, DH)
    key_out = lax.all_to_all(key_part[:, None, :], "seq", split_axis=0, concat_axis=1, tiled=True)
    key_sum = jnp.sum(
        key_out.reshape(tok_rows, kv_count, seq_ways // kv_count, DH).astype(jnp.float32), axis=2
    )
    key_final = key_sum.astype(jnp.bfloat16).reshape(tok_rows, kv_count * DH)
    return (pair_out[0][None], key_final[None], pair_out[1][None])


def solution(mesh):
    placed = (
        P("pipe", "seq", None),
        P("pipe", "seq", None),
        P("pipe", "seq", None),
        P("seq", None),
        P(),
    )
    return jax.shard_map(
        on_device,
        mesh=mesh,
        in_specs=placed,
        out_specs=(P("pipe", "seq", None), P("pipe", "seq", None), P("pipe", "seq", None)),
        check_vma=False,
    )
```

```python
import jax
import jax.numpy as jnp
from jax import lax
from jax.sharding import PartitionSpec as P

DH = 128
BLK = 128


def from_behind(value, axis, steps):
    count = lax.axis_size(axis)
    leading, last = (max(0, -steps), min(count, count - steps))
    return lax.ppermute(value, axis, [(source, source + steps) for source in range(leading, last)])


def key_pair(block_rows):
    first_block = jnp.broadcast_to(block_rows[:1], block_rows.shape)
    return jnp.concatenate([first_block, block_rows], axis=1)


def visible(lengths, block_count, block_len):
    shape = (block_count, block_len, 2 * block_len)
    row_index = lax.broadcasted_iota(jnp.int32, shape, 1)
    col_index = lax.broadcasted_iota(jnp.int32, shape, 2)
    block_index = lax.broadcasted_iota(jnp.int32, shape, 0)
    in_first = col_index < block_len
    offset = jnp.where(in_first, col_index, col_index - block_len)
    own_len = lengths[:, None, None]
    first_ok = in_first & (offset < lengths[0]) & ((block_index > 0) | (offset <= row_index))
    own_ok = (
        jnp.logical_not(in_first) & (block_index > 0) & (offset <= row_index) & (offset < own_len)
    )
    return (first_ok | own_ok)[:, None]


def fold_keys(key_terms, block_len):
    own_part = key_terms[:, block_len:]
    first_part = jnp.sum(key_terms[:, :block_len], axis=0)
    return own_part.at[0].add(first_part)


def fold_value(key_terms, block_len, groups):
    own_part = key_terms[:, block_len:]
    first_terms = key_terms[:, :block_len]
    grouped = first_terms.reshape((groups, first_terms.shape[0] // groups) + first_terms.shape[1:])
    partial_low = lax.optimization_barrier(jnp.sum(grouped, axis=1).astype(jnp.bfloat16))
    first_part = jnp.sum(partial_low.astype(jnp.float32), axis=0)
    return own_part.at[0].add(first_part)


def probabilities(query_blocks, keys_both, allowed, score_scale):
    scores = (
        jnp.einsum("bihd,bjhd->bhij", query_blocks, keys_both, preferred_element_type=jnp.float32)
        * score_scale
    )
    scores = jnp.where(allowed, scores, -jnp.inf)
    row_max = jnp.max(scores, axis=-1, keepdims=True)
    exp_scores = jnp.exp(scores - row_max)
    return exp_scores / jnp.sum(exp_scores, axis=-1, keepdims=True)


def value_grad(probs_low, grad_blocks, block_len, groups):
    key_terms = jnp.einsum(
        "bhij,bihd->bjhd", probs_low, grad_blocks, preferred_element_type=jnp.float32
    )
    return (grad_blocks.astype(jnp.float32) + fold_value(key_terms, block_len, groups)).astype(
        jnp.bfloat16
    )


def score_grads(
    softmax_probs, probs_low, query_blocks, keys_both, values_both, grad_blocks, score_scale
):
    output = jnp.einsum(
        "bhij,bjhd->bihd", probs_low, values_both, preferred_element_type=jnp.float32
    )
    row_dot = jnp.transpose(jnp.sum(grad_blocks.astype(jnp.float32) * output, axis=-1), (0, 2, 1))[
        ..., None
    ]
    grad_probs = jnp.einsum(
        "bihd,bjhd->bhij", grad_blocks, values_both, preferred_element_type=jnp.float32
    )
    grad_scores = (softmax_probs * (grad_probs - row_dot)).astype(jnp.bfloat16)
    grad_query = (
        jnp.einsum("bhij,bjhd->bihd", grad_scores, keys_both, preferred_element_type=jnp.float32)
        * score_scale
    ).astype(jnp.bfloat16)
    key_terms = jnp.einsum(
        "bhij,bihd->bjhd", grad_scores, query_blocks, preferred_element_type=jnp.float32
    )
    return (grad_query, key_terms)


def weight_grads(
    softmax_probs,
    probs_low,
    query_blocks,
    keys_both,
    values_both,
    grad_blocks,
    score_scale,
    block_len,
):
    grad_query, key_terms = score_grads(
        softmax_probs, probs_low, query_blocks, keys_both, values_both, grad_blocks, score_scale
    )
    grad_key = (fold_keys(key_terms, block_len) * score_scale).astype(jnp.bfloat16)
    return (grad_query, grad_key)


def on_device(queries, key_heads, inputs, cotangent, lengths):
    section_count = lax.axis_size("pipe")
    section_index = lax.axis_index("pipe")
    seq_ways = lax.axis_size("seq")
    seq_index = lax.axis_index("seq")
    tok_rows = queries.shape[1]
    full_width = queries.shape[2]
    head_count = full_width // DH
    kv_count = key_heads.shape[2] // DH
    group_size = head_count // kv_count
    seq_len = tok_rows * seq_ways
    block_count = seq_len // BLK
    local_heads = head_count // seq_ways
    score_scale = DH ** (-0.5)
    last_section = section_count - 1

    def to_heads(flat_rows):
        return flat_rows.reshape(block_count, BLK, local_heads, DH)

    def to_flat(block_rows):
        return block_rows.reshape(seq_len, local_heads * DH)

    def transpose_seq(value, split_axis, concat_axis, section=None):
        if seq_ways > 8:
            return lax.all_to_all(value, "seq", split_axis, concat_axis, tiled=True)
        split_size = value.shape[split_axis] // seq_ways
        concat_size = value.shape[concat_axis]
        out_shape = list(value.shape)
        out_shape[split_axis] = split_size
        out_shape[concat_axis] = concat_size * seq_ways
        result = jnp.zeros(out_shape, value.dtype)
        for shift in range(seq_ways):
            target = (seq_index + shift) % seq_ways
            chunk = lax.dynamic_slice_in_dim(value, target * split_size, split_size, axis=split_axis)
            if shift == 0:
                got = chunk
            elif section is None:
                got = lax.ppermute(
                    chunk, "seq", [(s, (s + shift) % seq_ways) for s in range(seq_ways)]
                )
            else:
                base = section * seq_ways
                got = lax.ppermute(
                    chunk,
                    ("pipe", "seq"),
                    [(base + s, base + (s + shift) % seq_ways) for s in range(seq_ways)],
                )
            source = (seq_index + seq_ways - shift) % seq_ways
            result = lax.dynamic_update_slice_in_dim(
                result, got, source * concat_size, axis=concat_axis
            )
        return result

    stacked_heads = transpose_seq(jnp.stack([queries[0], inputs[0]]), 2, 1)
    query_flat, input_flat = stacked_heads[0], stacked_heads[1]
    cot_flat = transpose_seq(cotangent, 1, 0, section=last_section)
    kv_pick = (jnp.arange(seq_ways) * local_heads) // group_size
    key_rows = key_heads[0].reshape(tok_rows, kv_count, DH)[:, kv_pick, :]
    key_flat = transpose_seq(key_rows, 1, 0)
    key_blocks = jnp.broadcast_to(
        key_flat.reshape(block_count, BLK, 1, DH), (block_count, BLK, local_heads, DH)
    )
    query_blocks = to_heads(query_flat)
    keys_both = key_pair(key_blocks)
    values_both = key_pair(to_heads(input_flat))
    allowed = visible(lengths, block_count, BLK)
    softmax_probs = probabilities(query_blocks, keys_both, allowed, score_scale)
    probs_low = softmax_probs.astype(jnp.bfloat16)

    def section_grads(grad_in):
        grad_query, grad_key = weight_grads(
            softmax_probs,
            probs_low,
            query_blocks,
            keys_both,
            values_both,
            to_heads(grad_in),
            score_scale,
            BLK,
        )
        if local_heads == 1:
            key_part = grad_key.reshape(seq_len, DH)
        else:
            key_part = jnp.sum(grad_key.astype(jnp.float32), axis=2).reshape(seq_len, DH)
        return (to_flat(grad_query), key_part)

    key_dtype = jnp.bfloat16 if local_heads == 1 else jnp.float32
    idle_grads = (
        jnp.zeros((seq_len, local_heads * DH), jnp.bfloat16),
        jnp.zeros((seq_len, DH), key_dtype),
    )

    arrived = jnp.zeros_like(cot_flat)
    pair_final = jnp.zeros((2, tok_rows, full_width), jnp.bfloat16)
    key_final = jnp.zeros((tok_rows, kv_count * DH), jnp.bfloat16)
    for tick in range(section_count):
        sender = last_section - tick
        active = section_index == sender
        grad_in = cot_flat if sender == last_section else arrived
        new_grad = to_flat(value_grad(probs_low, to_heads(grad_in), BLK, seq_ways))
        if sender > 0:
            arrived = lax.ppermute(new_grad, "pipe", [(sender, sender - 1)])
        grad_query, key_part = lax.cond(active, section_grads, lambda g: idle_grads, grad_in)
        pair_out = transpose_seq(jnp.stack([grad_query, new_grad]), 1, 2, section=sender)
        key_out = transpose_seq(key_part[:, None, :], 0, 1, section=sender)
        key_sum = jnp.sum(
            key_out.reshape(tok_rows, kv_count, seq_ways // kv_count, DH).astype(jnp.float32),
            axis=2,
        )
        pair_final = jnp.where(active, pair_out, pair_final)
        key_final = jnp.where(
            active, key_sum.astype(jnp.bfloat16).reshape(tok_rows, kv_count * DH), key_final
        )
    return (pair_final[0][None], key_final[None], pair_final[1][None])


def solution(mesh):
    placed = (
        P("pipe", "seq", None),
        P("pipe", "seq", None),
        P("pipe", "seq", None),
        P("seq", None),
        P(),
    )
    return jax.shard_map(
        on_device,
        mesh=mesh,
        in_specs=placed,
        out_specs=(P("pipe", "seq", None), P("pipe", "seq", None), P("pipe", "seq", None)),
        check_vma=False,
    )
```

```python
import jax
import jax.numpy as jnp
from jax import lax
from jax.sharding import PartitionSpec as P

DH = 128
BLK = 128


def key_pair(block_rows):
    first_block = jnp.broadcast_to(block_rows[:, :1], block_rows.shape)
    return jnp.concatenate([first_block, block_rows], axis=2)


def visible(lengths, block_count, block_len):
    shape = (block_count, block_len, 2 * block_len)
    row_index = lax.broadcasted_iota(jnp.int32, shape, 1)
    col_index = lax.broadcasted_iota(jnp.int32, shape, 2)
    block_index = lax.broadcasted_iota(jnp.int32, shape, 0)
    in_first = col_index < block_len
    offset = jnp.where(in_first, col_index, col_index - block_len)
    own_len = lengths[:, None, None]
    first_ok = in_first & (offset < lengths[0]) & ((block_index > 0) | (offset <= row_index))
    own_ok = (
        jnp.logical_not(in_first) & (block_index > 0) & (offset <= row_index) & (offset < own_len)
    )
    return (first_ok | own_ok)[None]


def fold_keys(key_terms, block_len):
    own_part = key_terms[:, :, block_len:]
    first_part = jnp.sum(key_terms[:, :, :block_len], axis=1)
    return own_part.at[:, 0].add(first_part)


def fold_value(key_terms, block_len, groups):
    own_part = key_terms[:, :, block_len:]
    first_terms = key_terms[:, :, :block_len]
    heads, blocks = first_terms.shape[:2]
    grouped = first_terms.reshape((heads, groups, blocks // groups) + first_terms.shape[2:])
    partial_low = lax.optimization_barrier(jnp.sum(grouped, axis=2).astype(jnp.bfloat16))
    first_part = jnp.sum(partial_low.astype(jnp.float32), axis=1)
    return own_part.at[:, 0].add(first_part)


def probabilities(query_blocks, keys_both, allowed, score_scale):
    scores = (
        jnp.einsum("hbid,hbjd->hbij", query_blocks, keys_both, preferred_element_type=jnp.float32)
        * score_scale
    )
    scores = jnp.where(allowed, scores, -jnp.inf)
    row_max = jnp.max(scores, axis=-1, keepdims=True)
    exp_scores = jnp.exp(scores - row_max)
    return exp_scores / jnp.sum(exp_scores, axis=-1, keepdims=True)


def value_grad(probs_low, grad_blocks, block_len, groups):
    key_terms = jnp.einsum(
        "hbij,hbid->hbjd", probs_low, grad_blocks, preferred_element_type=jnp.float32
    )
    return (grad_blocks.astype(jnp.float32) + fold_value(key_terms, block_len, groups)).astype(
        jnp.bfloat16
    )


def weight_grads(
    softmax_probs, probs_low, query_blocks, keys_both, values_both, grad_blocks, score_scale, block_len
):
    output = jnp.einsum(
        "hbij,hbjd->hbid", probs_low, values_both, preferred_element_type=jnp.float32
    )
    row_dot = jnp.sum(grad_blocks.astype(jnp.float32) * output, axis=-1)[..., None]
    grad_probs = jnp.einsum(
        "hbid,hbjd->hbij", grad_blocks, values_both, preferred_element_type=jnp.float32
    )
    grad_scores = (softmax_probs * (grad_probs - row_dot)).astype(jnp.bfloat16)
    grad_query = (
        jnp.einsum("hbij,hbjd->hbid", grad_scores, keys_both, preferred_element_type=jnp.float32)
        * score_scale
    ).astype(jnp.bfloat16)
    key_terms = jnp.einsum(
        "hbij,hbid->hbjd", grad_scores, query_blocks, preferred_element_type=jnp.float32
    )
    grad_key = (fold_keys(key_terms, block_len) * score_scale).astype(jnp.bfloat16)
    return (grad_query, grad_key)


def on_device(queries, key_heads, inputs, cotangent, lengths):
    section_count = lax.axis_size("pipe")
    section_index = lax.axis_index("pipe")
    seq_ways = lax.axis_size("seq")
    tok_rows = queries.shape[1]
    full_width = queries.shape[2]
    head_count = full_width // DH
    kv_count = key_heads.shape[2] // DH
    group_size = head_count // kv_count
    seq_len = tok_rows * seq_ways
    block_count = seq_len // BLK
    local_heads = head_count // seq_ways
    score_scale = DH ** (-0.5)
    last_section = section_count - 1

    def to_blocks(head_rows):
        return head_rows.reshape(local_heads, block_count, BLK, DH)

    def head_major(rows):
        return jnp.transpose(rows.reshape(tok_rows, head_count, DH), (1, 0, 2))

    stacked = jnp.stack([head_major(queries[0]), head_major(inputs[0]), head_major(cotangent)])
    stacked_heads = lax.all_to_all(stacked, "seq", split_axis=1, concat_axis=2, tiled=True)
    query_blocks = to_blocks(stacked_heads[0])
    values_both = key_pair(to_blocks(stacked_heads[1]))
    cot_blocks = to_blocks(stacked_heads[2])
    kv_pick = (jnp.arange(seq_ways) * local_heads) // group_size
    key_rows = jnp.transpose(key_heads[0].reshape(tok_rows, kv_count, DH), (1, 0, 2))[kv_pick]
    key_flat = lax.all_to_all(key_rows, "seq", split_axis=0, concat_axis=1, tiled=True)
    key_blocks = jnp.broadcast_to(
        key_flat.reshape(1, block_count, BLK, DH), (local_heads, block_count, BLK, DH)
    )
    keys_both = key_pair(key_blocks)
    allowed = visible(lengths, block_count, BLK)
    softmax_probs = probabilities(query_blocks, keys_both, allowed, score_scale)
    probs_low = softmax_probs.astype(jnp.bfloat16)

    grad_ins = []
    grad_outs = []
    grad_in = cot_blocks
    for tick in range(section_count):
        sender = last_section - tick
        new_grad = value_grad(probs_low, grad_in, BLK, seq_ways)
        grad_ins.append(grad_in)
        grad_outs.append(new_grad)
        if sender > 0:
            grad_in = lax.ppermute(new_grad, "pipe", [(sender, sender - 1)])

    def by_section(per_tick):
        chosen = per_tick[0]
        for tick in range(1, section_count):
            chosen = jnp.where(section_index == last_section - tick, per_tick[tick], chosen)
        return chosen

    held_in = by_section(grad_ins)
    held_out = by_section(grad_outs)
    grad_query, grad_key = weight_grads(
        softmax_probs,
        probs_low,
        query_blocks,
        keys_both,
        values_both,
        held_in,
        score_scale,
        BLK,
    )
    pair = jnp.stack([grad_query, held_out]).reshape(2, local_heads, seq_len, DH)
    pair_out = lax.all_to_all(pair, "seq", split_axis=2, concat_axis=1, tiled=True)
    pair_rows = jnp.transpose(pair_out, (0, 2, 1, 3)).reshape(2, tok_rows, full_width)
    if local_heads == 1:
        key_part = grad_key.reshape(seq_len, DH)
    else:
        key_part = jnp.sum(grad_key.astype(jnp.float32), axis=0).reshape(seq_len, DH)
    key_out = lax.all_to_all(key_part[:, None, :], "seq", split_axis=0, concat_axis=1, tiled=True)
    key_sum = jnp.sum(
        key_out.reshape(tok_rows, kv_count, seq_ways // kv_count, DH).astype(jnp.float32), axis=2
    )
    key_final = key_sum.astype(jnp.bfloat16).reshape(tok_rows, kv_count * DH)
    return (pair_rows[0][None], key_final[None], pair_rows[1][None])


def solution(mesh):
    placed = (
        P("pipe", "seq", None),
        P("pipe", "seq", None),
        P("pipe", "seq", None),
        P("seq", None),
        P(),
    )
    return jax.shard_map(
        on_device,
        mesh=mesh,
        in_specs=placed,
        out_specs=(P("pipe", "seq", None), P("pipe", "seq", None), P("pipe", "seq", None)),
        check_vma=False,
    )
```

```python
import jax
import jax.numpy as jnp
from jax import lax
from jax.sharding import PartitionSpec as P

DH = 128
BLK = 128


def key_pair(block_rows):
    first_block = jnp.broadcast_to(block_rows[:, :1], block_rows.shape)
    return jnp.concatenate([first_block, block_rows], axis=2)


def visible(lengths, block_count, block_len):
    shape = (block_count, block_len, 2 * block_len)
    row_index = lax.broadcasted_iota(jnp.int32, shape, 1)
    col_index = lax.broadcasted_iota(jnp.int32, shape, 2)
    block_index = lax.broadcasted_iota(jnp.int32, shape, 0)
    in_first = col_index < block_len
    offset = jnp.where(in_first, col_index, col_index - block_len)
    own_len = lengths[:, None, None]
    first_ok = in_first & (offset < lengths[0]) & ((block_index > 0) | (offset <= row_index))
    own_ok = (
        jnp.logical_not(in_first) & (block_index > 0) & (offset <= row_index) & (offset < own_len)
    )
    return (first_ok | own_ok)[None]


def fold_keys(key_terms, block_len):
    own_part = key_terms[:, :, block_len:]
    first_part = jnp.sum(key_terms[:, :, :block_len], axis=1)
    return own_part.at[:, 0].add(first_part)


def fold_value(key_terms, block_len, groups):
    own_part = key_terms[:, :, block_len:]
    first_terms = key_terms[:, :, :block_len]
    heads, blocks = first_terms.shape[:2]
    grouped = first_terms.reshape((heads, groups, blocks // groups) + first_terms.shape[2:])
    partial_low = lax.optimization_barrier(jnp.sum(grouped, axis=2).astype(jnp.bfloat16))
    first_part = jnp.sum(partial_low.astype(jnp.float32), axis=1)
    return own_part.at[:, 0].add(first_part)


def probabilities(query_blocks, keys_both, allowed, score_scale):
    scores = (
        jnp.einsum("hbid,hbjd->hbij", query_blocks, keys_both, preferred_element_type=jnp.float32)
        * score_scale
    )
    scores = jnp.where(allowed, scores, -jnp.inf)
    row_max = jnp.max(scores, axis=-1, keepdims=True)
    exp_scores = jnp.exp(scores - row_max)
    return exp_scores / jnp.sum(exp_scores, axis=-1, keepdims=True)


def value_grad(probs_low, grad_blocks, block_len, groups):
    key_terms = jnp.einsum(
        "hbij,hbid->hbjd", probs_low, grad_blocks, preferred_element_type=jnp.float32
    )
    return (grad_blocks.astype(jnp.float32) + fold_value(key_terms, block_len, groups)).astype(
        jnp.bfloat16
    )


def weight_grads(
    softmax_probs, probs_low, query_blocks, keys_both, values_both, grad_blocks, score_scale, block_len
):
    output = jnp.einsum(
        "hbij,hbjd->hbid", probs_low, values_both, preferred_element_type=jnp.float32
    )
    row_dot = jnp.sum(grad_blocks.astype(jnp.float32) * output, axis=-1)[..., None]
    grad_probs = jnp.einsum(
        "hbid,hbjd->hbij", grad_blocks, values_both, preferred_element_type=jnp.float32
    )
    grad_scores = (softmax_probs * (grad_probs - row_dot)).astype(jnp.bfloat16)
    grad_query = (
        jnp.einsum("hbij,hbjd->hbid", grad_scores, keys_both, preferred_element_type=jnp.float32)
        * score_scale
    ).astype(jnp.bfloat16)
    key_terms = jnp.einsum(
        "hbij,hbid->hbjd", grad_scores, query_blocks, preferred_element_type=jnp.float32
    )
    grad_key = (fold_keys(key_terms, block_len) * score_scale).astype(jnp.bfloat16)
    return (grad_query, grad_key)


def on_device(queries, key_heads, inputs, cotangent, lengths):
    section_count = lax.axis_size("pipe")
    section_index = lax.axis_index("pipe")
    seq_ways = lax.axis_size("seq")
    tok_rows = queries.shape[1]
    full_width = queries.shape[2]
    head_count = full_width // DH
    kv_count = key_heads.shape[2] // DH
    group_size = head_count // kv_count
    seq_len = tok_rows * seq_ways
    block_count = seq_len // BLK
    local_heads = head_count // seq_ways
    score_scale = DH ** (-0.5)
    last_section = section_count - 1

    def to_blocks(head_rows):
        return head_rows.reshape(local_heads, block_count, BLK, DH)

    def head_major(rows):
        return jnp.transpose(rows.reshape(tok_rows, head_count, DH), (1, 0, 2))

    stacked = jnp.stack([head_major(queries[0]), head_major(cotangent)])
    stacked_heads = lax.all_to_all(stacked, "seq", split_axis=1, concat_axis=2, tiled=True)
    query_blocks = to_blocks(stacked_heads[0])
    cot_blocks = to_blocks(stacked_heads[1])
    input_heads = lax.all_to_all(head_major(inputs[0]), "seq", split_axis=0, concat_axis=1, tiled=True)
    values_both = key_pair(to_blocks(input_heads))
    kv_pick = (jnp.arange(seq_ways) * local_heads) // group_size
    key_rows = jnp.transpose(key_heads[0].reshape(tok_rows, kv_count, DH), (1, 0, 2))[kv_pick]
    key_flat = lax.all_to_all(key_rows, "seq", split_axis=0, concat_axis=1, tiled=True)
    key_blocks = jnp.broadcast_to(
        key_flat.reshape(1, block_count, BLK, DH), (local_heads, block_count, BLK, DH)
    )
    keys_both = key_pair(key_blocks)
    allowed = visible(lengths, block_count, BLK)
    softmax_probs = probabilities(query_blocks, keys_both, allowed, score_scale)
    probs_low = softmax_probs.astype(jnp.bfloat16)

    grad_ins = []
    grad_outs = []
    grad_in = cot_blocks
    for tick in range(section_count):
        sender = last_section - tick
        new_grad = value_grad(probs_low, grad_in, BLK, seq_ways)
        grad_ins.append(grad_in)
        grad_outs.append(new_grad)
        if sender > 0:
            grad_in = lax.ppermute(new_grad, "pipe", [(sender, sender - 1)])

    def by_section(per_tick):
        chosen = per_tick[0]
        for tick in range(1, section_count):
            chosen = jnp.where(section_index == last_section - tick, per_tick[tick], chosen)
        return chosen

    held_in = by_section(grad_ins)
    held_out = by_section(grad_outs)
    grad_out = lax.all_to_all(
        held_out.reshape(local_heads, seq_len, DH), "seq", split_axis=1, concat_axis=0, tiled=True
    )
    grad_rows = jnp.transpose(grad_out, (1, 0, 2)).reshape(tok_rows, full_width)
    grad_query, grad_key = weight_grads(
        softmax_probs,
        probs_low,
        query_blocks,
        keys_both,
        values_both,
        held_in,
        score_scale,
        BLK,
    )
    query_out = lax.all_to_all(
        grad_query.reshape(local_heads, seq_len, DH), "seq", split_axis=1, concat_axis=0, tiled=True
    )
    query_rows = jnp.transpose(query_out, (1, 0, 2)).reshape(tok_rows, full_width)
    if local_heads == 1:
        key_part = grad_key.reshape(seq_len, DH)
    else:
        key_part = jnp.sum(grad_key.astype(jnp.float32), axis=0).reshape(seq_len, DH)
    key_out = lax.all_to_all(key_part[:, None, :], "seq", split_axis=0, concat_axis=1, tiled=True)
    key_sum = jnp.sum(
        key_out.reshape(tok_rows, kv_count, seq_ways // kv_count, DH).astype(jnp.float32), axis=2
    )
    key_final = key_sum.astype(jnp.bfloat16).reshape(tok_rows, kv_count * DH)
    return (query_rows[None], key_final[None], grad_rows[None])


def solution(mesh):
    placed = (
        P("pipe", "seq", None),
        P("pipe", "seq", None),
        P("pipe", "seq", None),
        P("seq", None),
        P(),
    )
    return jax.shard_map(
        on_device,
        mesh=mesh,
        in_specs=placed,
        out_specs=(P("pipe", "seq", None), P("pipe", "seq", None), P("pipe", "seq", None)),
        check_vma=False,
    )
```

```python
import jax
import jax.numpy as jnp
from jax import lax
from jax.sharding import PartitionSpec as P

DH = 128
BLK = 128


def key_pair(block_rows):
    first_block = jnp.broadcast_to(block_rows[:, :1], block_rows.shape)
    return jnp.concatenate([first_block, block_rows], axis=2)


def visible(lengths, block_count, block_len):
    shape = (block_count, block_len, 2 * block_len)
    row_index = lax.broadcasted_iota(jnp.int32, shape, 1)
    col_index = lax.broadcasted_iota(jnp.int32, shape, 2)
    block_index = lax.broadcasted_iota(jnp.int32, shape, 0)
    in_first = col_index < block_len
    offset = jnp.where(in_first, col_index, col_index - block_len)
    own_len = lengths[:, None, None]
    first_ok = in_first & (offset < lengths[0]) & ((block_index > 0) | (offset <= row_index))
    own_ok = (
        jnp.logical_not(in_first) & (block_index > 0) & (offset <= row_index) & (offset < own_len)
    )
    return (first_ok | own_ok)[None]


def fold_keys(key_terms, block_len):
    own_part = key_terms[:, :, block_len:]
    first_part = jnp.sum(key_terms[:, :, :block_len], axis=1)
    return own_part.at[:, 0].add(first_part)


def fold_value(key_terms, block_len, groups):
    own_part = key_terms[:, :, block_len:]
    first_terms = key_terms[:, :, :block_len]
    heads, blocks = first_terms.shape[:2]
    grouped = first_terms.reshape((heads, groups, blocks // groups) + first_terms.shape[2:])
    partial_low = lax.optimization_barrier(jnp.sum(grouped, axis=2).astype(jnp.bfloat16))
    first_part = jnp.sum(partial_low.astype(jnp.float32), axis=1)
    return own_part.at[:, 0].add(first_part)


def probabilities(query_blocks, keys_both, allowed, score_scale):
    scores = (
        jnp.einsum("hbid,hbjd->hbij", query_blocks, keys_both, preferred_element_type=jnp.float32)
        * score_scale
    )
    scores = jnp.where(allowed, scores, -jnp.inf)
    row_max = jnp.max(scores, axis=-1, keepdims=True)
    exp_scores = jnp.exp(scores - row_max)
    return exp_scores / jnp.sum(exp_scores, axis=-1, keepdims=True)


def value_grad(probs_low, grad_blocks, block_len, groups):
    key_terms = jnp.einsum(
        "hbij,hbid->hbjd", probs_low, grad_blocks, preferred_element_type=jnp.float32
    )
    return (grad_blocks.astype(jnp.float32) + fold_value(key_terms, block_len, groups)).astype(
        jnp.bfloat16
    )


def weight_grads(
    softmax_probs, probs_low, query_blocks, keys_both, values_both, grad_blocks, score_scale, block_len
):
    output = jnp.einsum(
        "hbij,hbjd->hbid", probs_low, values_both, preferred_element_type=jnp.float32
    )
    row_dot = jnp.sum(grad_blocks.astype(jnp.float32) * output, axis=-1)[..., None]
    grad_probs = jnp.einsum(
        "hbid,hbjd->hbij", grad_blocks, values_both, preferred_element_type=jnp.float32
    )
    grad_scores = (softmax_probs * (grad_probs - row_dot)).astype(jnp.bfloat16)
    grad_query = (
        jnp.einsum("hbij,hbjd->hbid", grad_scores, keys_both, preferred_element_type=jnp.float32)
        * score_scale
    ).astype(jnp.bfloat16)
    key_terms = jnp.einsum(
        "hbij,hbid->hbjd", grad_scores, query_blocks, preferred_element_type=jnp.float32
    )
    grad_key = (fold_keys(key_terms, block_len) * score_scale).astype(jnp.bfloat16)
    return (grad_query, grad_key)


def on_device(queries, key_heads, inputs, cotangent, lengths):
    section_count = lax.axis_size("pipe")
    section_index = lax.axis_index("pipe")
    seq_ways = lax.axis_size("seq")
    tok_rows = queries.shape[1]
    full_width = queries.shape[2]
    head_count = full_width // DH
    kv_count = key_heads.shape[2] // DH
    group_size = head_count // kv_count
    seq_len = tok_rows * seq_ways
    block_count = seq_len // BLK
    local_heads = head_count // seq_ways
    score_scale = DH ** (-0.5)
    last_section = section_count - 1

    seq_index = lax.axis_index("seq")

    def transpose_seq(value, split_axis, concat_axis):
        if seq_ways > 8:
            return lax.all_to_all(value, "seq", split_axis, concat_axis, tiled=True)
        split_size = value.shape[split_axis] // seq_ways
        concat_size = value.shape[concat_axis]
        out_shape = list(value.shape)
        out_shape[split_axis] = split_size
        out_shape[concat_axis] = concat_size * seq_ways
        result = jnp.zeros(out_shape, value.dtype)
        for shift in range(seq_ways):
            target = (seq_index + shift) % seq_ways
            chunk = lax.dynamic_slice_in_dim(value, target * split_size, split_size, axis=split_axis)
            if shift > 0:
                chunk = lax.ppermute(
                    chunk, "seq", [(s, (s + shift) % seq_ways) for s in range(seq_ways)]
                )
            source = (seq_index + seq_ways - shift) % seq_ways
            result = lax.dynamic_update_slice_in_dim(
                result, chunk, source * concat_size, axis=concat_axis
            )
        return result

    def to_blocks(head_rows):
        return head_rows.reshape(local_heads, block_count, BLK, DH)

    def head_major(rows):
        return jnp.transpose(rows.reshape(tok_rows, head_count, DH), (1, 0, 2))

    stacked = jnp.stack([head_major(queries[0]), head_major(cotangent)])
    stacked_heads = transpose_seq(stacked, 1, 2)
    query_blocks = to_blocks(stacked_heads[0])
    cot_blocks = to_blocks(stacked_heads[1])
    input_heads = lax.all_to_all(head_major(inputs[0]), "seq", split_axis=0, concat_axis=1, tiled=True)
    values_both = key_pair(to_blocks(input_heads))
    kv_pick = (jnp.arange(seq_ways) * local_heads) // group_size
    key_rows = jnp.transpose(key_heads[0].reshape(tok_rows, kv_count, DH), (1, 0, 2))[kv_pick]
    key_flat = lax.all_to_all(key_rows, "seq", split_axis=0, concat_axis=1, tiled=True)
    key_blocks = jnp.broadcast_to(
        key_flat.reshape(1, block_count, BLK, DH), (local_heads, block_count, BLK, DH)
    )
    keys_both = key_pair(key_blocks)
    allowed = visible(lengths, block_count, BLK)
    softmax_probs = probabilities(query_blocks, keys_both, allowed, score_scale)
    probs_low = softmax_probs.astype(jnp.bfloat16)

    grad_ins = []
    grad_outs = []
    grad_in = cot_blocks
    for tick in range(section_count):
        sender = last_section - tick
        new_grad = value_grad(probs_low, grad_in, BLK, seq_ways)
        grad_ins.append(grad_in)
        grad_outs.append(new_grad)
        if sender > 0:
            grad_in = lax.ppermute(new_grad, "pipe", [(sender, sender - 1)])

    def by_section(per_tick):
        chosen = per_tick[0]
        for tick in range(1, section_count):
            chosen = jnp.where(section_index == last_section - tick, per_tick[tick], chosen)
        return chosen

    held_in = by_section(grad_ins)
    held_out = by_section(grad_outs)
    grad_query, grad_key = weight_grads(
        softmax_probs,
        probs_low,
        query_blocks,
        keys_both,
        values_both,
        held_in,
        score_scale,
        BLK,
    )
    pair = jnp.stack([grad_query, held_out]).reshape(2, local_heads, seq_len, DH)
    pair_out = transpose_seq(pair, 2, 1)
    pair_rows = jnp.transpose(pair_out, (0, 2, 1, 3)).reshape(2, tok_rows, full_width)
    if local_heads == 1:
        key_part = grad_key.reshape(seq_len, DH)
    else:
        key_part = jnp.sum(grad_key.astype(jnp.float32), axis=0).reshape(seq_len, DH)
    key_out = lax.all_to_all(key_part[:, None, :], "seq", split_axis=0, concat_axis=1, tiled=True)
    key_sum = jnp.sum(
        key_out.reshape(tok_rows, kv_count, seq_ways // kv_count, DH).astype(jnp.float32), axis=2
    )
    key_final = key_sum.astype(jnp.bfloat16).reshape(tok_rows, kv_count * DH)
    return (pair_rows[0][None], key_final[None], pair_rows[1][None])


def solution(mesh):
    placed = (
        P("pipe", "seq", None),
        P("pipe", "seq", None),
        P("pipe", "seq", None),
        P("seq", None),
        P(),
    )
    return jax.shard_map(
        on_device,
        mesh=mesh,
        in_specs=placed,
        out_specs=(P("pipe", "seq", None), P("pipe", "seq", None), P("pipe", "seq", None)),
        check_vma=False,
    )
```

```python
import jax
import jax.numpy as jnp
from jax import lax
from jax.sharding import PartitionSpec as P

DH = 128
BLK = 128


def key_pair(block_rows):
    first_block = jnp.broadcast_to(block_rows[:, :1], block_rows.shape)
    return jnp.concatenate([first_block, block_rows], axis=2)


def visible(lengths, block_count, block_len):
    shape = (block_count, block_len, 2 * block_len)
    row_index = lax.broadcasted_iota(jnp.int32, shape, 1)
    col_index = lax.broadcasted_iota(jnp.int32, shape, 2)
    block_index = lax.broadcasted_iota(jnp.int32, shape, 0)
    in_first = col_index < block_len
    offset = jnp.where(in_first, col_index, col_index - block_len)
    own_len = lengths[:, None, None]
    first_ok = in_first & (offset < lengths[0]) & ((block_index > 0) | (offset <= row_index))
    own_ok = (
        jnp.logical_not(in_first) & (block_index > 0) & (offset <= row_index) & (offset < own_len)
    )
    return (first_ok | own_ok)[None]


def fold_keys(key_terms, block_len):
    own_part = key_terms[:, :, block_len:]
    first_part = jnp.sum(key_terms[:, :, :block_len], axis=1)
    return own_part.at[:, 0].add(first_part)


def fold_value(key_terms, block_len, groups):
    own_part = key_terms[:, :, block_len:]
    first_terms = key_terms[:, :, :block_len]
    heads, blocks = first_terms.shape[:2]
    grouped = first_terms.reshape((heads, groups, blocks // groups) + first_terms.shape[2:])
    partial_low = lax.optimization_barrier(jnp.sum(grouped, axis=2).astype(jnp.bfloat16))
    first_part = jnp.sum(partial_low.astype(jnp.float32), axis=1)
    return own_part.at[:, 0].add(first_part)


def probabilities(query_blocks, keys_both, allowed, score_scale):
    scores = (
        jnp.einsum("hbid,hbjd->hbij", query_blocks, keys_both, preferred_element_type=jnp.float32)
        * score_scale
    )
    scores = jnp.where(allowed, scores, -jnp.inf)
    row_max = jnp.max(scores, axis=-1, keepdims=True)
    exp_scores = jnp.exp(scores - row_max)
    return exp_scores / jnp.sum(exp_scores, axis=-1, keepdims=True)


def value_grad(probs_low, grad_blocks, block_len, groups):
    key_terms = jnp.einsum(
        "hbij,hbid->hbjd", probs_low, grad_blocks, preferred_element_type=jnp.float32
    )
    return (grad_blocks.astype(jnp.float32) + fold_value(key_terms, block_len, groups)).astype(
        jnp.bfloat16
    )


def weight_grads(
    softmax_probs, probs_low, query_blocks, keys_both, values_both, grad_blocks, score_scale, block_len
):
    output = jnp.einsum(
        "hbij,hbjd->hbid", probs_low, values_both, preferred_element_type=jnp.float32
    )
    row_dot = jnp.sum(grad_blocks.astype(jnp.float32) * output, axis=-1)[..., None]
    grad_probs = jnp.einsum(
        "hbid,hbjd->hbij", grad_blocks, values_both, preferred_element_type=jnp.float32
    )
    grad_scores = (softmax_probs * (grad_probs - row_dot)).astype(jnp.bfloat16)
    grad_query = (
        jnp.einsum("hbij,hbjd->hbid", grad_scores, keys_both, preferred_element_type=jnp.float32)
        * score_scale
    ).astype(jnp.bfloat16)
    key_terms = jnp.einsum(
        "hbij,hbid->hbjd", grad_scores, query_blocks, preferred_element_type=jnp.float32
    )
    grad_key = (fold_keys(key_terms, block_len) * score_scale).astype(jnp.bfloat16)
    return (grad_query, grad_key)


def on_device(queries, key_heads, inputs, cotangent, lengths):
    section_count = lax.axis_size("pipe")
    section_index = lax.axis_index("pipe")
    seq_ways = lax.axis_size("seq")
    tok_rows = queries.shape[1]
    full_width = queries.shape[2]
    head_count = full_width // DH
    kv_count = key_heads.shape[2] // DH
    group_size = head_count // kv_count
    seq_len = tok_rows * seq_ways
    block_count = seq_len // BLK
    local_heads = head_count // seq_ways
    score_scale = DH ** (-0.5)
    last_section = section_count - 1

    seq_index = lax.axis_index("seq")

    def transpose_seq(value, split_axis, concat_axis):
        if seq_ways > 8:
            return lax.all_to_all(value, "seq", split_axis, concat_axis, tiled=True)
        split_size = value.shape[split_axis] // seq_ways
        concat_size = value.shape[concat_axis]
        out_shape = list(value.shape)
        out_shape[split_axis] = split_size
        out_shape[concat_axis] = concat_size * seq_ways
        result = jnp.zeros(out_shape, value.dtype)
        for shift in range(seq_ways):
            target = (seq_index + shift) % seq_ways
            chunk = lax.dynamic_slice_in_dim(value, target * split_size, split_size, axis=split_axis)
            if shift > 0:
                chunk = lax.ppermute(
                    chunk, "seq", [(s, (s + shift) % seq_ways) for s in range(seq_ways)]
                )
            source = (seq_index + seq_ways - shift) % seq_ways
            result = lax.dynamic_update_slice_in_dim(
                result, chunk, source * concat_size, axis=concat_axis
            )
        return result

    def to_blocks(head_rows):
        return head_rows.reshape(local_heads, block_count, BLK, DH)

    def head_major(rows):
        return jnp.transpose(rows.reshape(tok_rows, head_count, DH), (1, 0, 2))

    stacked = jnp.stack([head_major(queries[0]), head_major(cotangent)])
    stacked_heads = transpose_seq(stacked, 1, 2)
    query_blocks = to_blocks(stacked_heads[0])
    cot_blocks = to_blocks(stacked_heads[1])
    input_heads = transpose_seq(head_major(inputs[0]), 0, 1)
    values_both = key_pair(to_blocks(input_heads))
    kv_pick = (jnp.arange(seq_ways) * local_heads) // group_size
    key_rows = jnp.transpose(key_heads[0].reshape(tok_rows, kv_count, DH), (1, 0, 2))[kv_pick]
    key_flat = lax.all_to_all(key_rows, "seq", split_axis=0, concat_axis=1, tiled=True)
    key_blocks = jnp.broadcast_to(
        key_flat.reshape(1, block_count, BLK, DH), (local_heads, block_count, BLK, DH)
    )
    keys_both = key_pair(key_blocks)
    allowed = visible(lengths, block_count, BLK)
    softmax_probs = probabilities(query_blocks, keys_both, allowed, score_scale)
    probs_low = softmax_probs.astype(jnp.bfloat16)

    grad_ins = []
    grad_outs = []
    grad_in = cot_blocks
    for tick in range(section_count):
        sender = last_section - tick
        new_grad = value_grad(probs_low, grad_in, BLK, seq_ways)
        grad_ins.append(grad_in)
        grad_outs.append(new_grad)
        if sender > 0:
            grad_in = lax.ppermute(new_grad, "pipe", [(sender, sender - 1)])

    def by_section(per_tick):
        chosen = per_tick[0]
        for tick in range(1, section_count):
            chosen = jnp.where(section_index == last_section - tick, per_tick[tick], chosen)
        return chosen

    held_in = by_section(grad_ins)
    held_out = by_section(grad_outs)
    grad_query, grad_key = weight_grads(
        softmax_probs,
        probs_low,
        query_blocks,
        keys_both,
        values_both,
        held_in,
        score_scale,
        BLK,
    )
    pair = jnp.stack([grad_query, held_out]).reshape(2, local_heads, seq_len, DH)
    pair_out = transpose_seq(pair, 2, 1)
    pair_rows = jnp.transpose(pair_out, (0, 2, 1, 3)).reshape(2, tok_rows, full_width)
    if local_heads == 1:
        key_part = grad_key.reshape(seq_len, DH)
    else:
        key_part = jnp.sum(grad_key.astype(jnp.float32), axis=0).reshape(seq_len, DH)
    key_out = lax.all_to_all(key_part[:, None, :], "seq", split_axis=0, concat_axis=1, tiled=True)
    key_sum = jnp.sum(
        key_out.reshape(tok_rows, kv_count, seq_ways // kv_count, DH).astype(jnp.float32), axis=2
    )
    key_final = key_sum.astype(jnp.bfloat16).reshape(tok_rows, kv_count * DH)
    return (pair_rows[0][None], key_final[None], pair_rows[1][None])


def solution(mesh):
    placed = (
        P("pipe", "seq", None),
        P("pipe", "seq", None),
        P("pipe", "seq", None),
        P("seq", None),
        P(),
    )
    return jax.shard_map(
        on_device,
        mesh=mesh,
        in_specs=placed,
        out_specs=(P("pipe", "seq", None), P("pipe", "seq", None), P("pipe", "seq", None)),
        check_vma=False,
    )
```

```python
import jax
import jax.numpy as jnp
from jax import lax
from jax.sharding import PartitionSpec as P

DH = 128
BLK = 128


def key_pair(block_rows):
    first_block = jnp.broadcast_to(block_rows[:, :1], block_rows.shape)
    return jnp.concatenate([first_block, block_rows], axis=2)


def visible(lengths, block_count, block_len):
    shape = (block_count, block_len, 2 * block_len)
    row_index = lax.broadcasted_iota(jnp.int32, shape, 1)
    col_index = lax.broadcasted_iota(jnp.int32, shape, 2)
    block_index = lax.broadcasted_iota(jnp.int32, shape, 0)
    in_first = col_index < block_len
    offset = jnp.where(in_first, col_index, col_index - block_len)
    own_len = lengths[:, None, None]
    first_ok = in_first & (offset < lengths[0]) & ((block_index > 0) | (offset <= row_index))
    own_ok = (
        jnp.logical_not(in_first) & (block_index > 0) & (offset <= row_index) & (offset < own_len)
    )
    return (first_ok | own_ok)[None]


def fold_keys(key_terms, block_len):
    own_part = key_terms[:, :, block_len:]
    first_part = jnp.sum(key_terms[:, :, :block_len], axis=1)
    return own_part.at[:, 0].add(first_part)


def fold_value(key_terms, block_len, groups):
    own_part = key_terms[:, :, block_len:]
    first_terms = key_terms[:, :, :block_len]
    heads, blocks = first_terms.shape[:2]
    grouped = first_terms.reshape((heads, groups, blocks // groups) + first_terms.shape[2:])
    partial_low = lax.optimization_barrier(jnp.sum(grouped, axis=2).astype(jnp.bfloat16))
    first_part = jnp.sum(partial_low.astype(jnp.float32), axis=1)
    return own_part.at[:, 0].add(first_part)


def probabilities(query_blocks, keys_both, allowed, score_scale):
    scores = (
        jnp.einsum("hbid,hbjd->hbij", query_blocks, keys_both, preferred_element_type=jnp.float32)
        * score_scale
    )
    scores = jnp.where(allowed, scores, -jnp.inf)
    row_max = jnp.max(scores, axis=-1, keepdims=True)
    exp_scores = jnp.exp(scores - row_max)
    return exp_scores / jnp.sum(exp_scores, axis=-1, keepdims=True)


def value_grad(probs_low, grad_blocks, block_len, groups):
    key_terms = jnp.einsum(
        "hbij,hbid->hbjd", probs_low, grad_blocks, preferred_element_type=jnp.float32
    )
    return (grad_blocks.astype(jnp.float32) + fold_value(key_terms, block_len, groups)).astype(
        jnp.bfloat16
    )


def weight_grads(
    softmax_probs, probs_low, query_blocks, keys_both, values_both, grad_blocks, score_scale, block_len
):
    output = jnp.einsum(
        "hbij,hbjd->hbid", probs_low, values_both, preferred_element_type=jnp.float32
    )
    row_dot = jnp.sum(grad_blocks.astype(jnp.float32) * output, axis=-1)[..., None]
    grad_probs = jnp.einsum(
        "hbid,hbjd->hbij", grad_blocks, values_both, preferred_element_type=jnp.float32
    )
    grad_scores = (softmax_probs * (grad_probs - row_dot)).astype(jnp.bfloat16)
    grad_query = (
        jnp.einsum("hbij,hbjd->hbid", grad_scores, keys_both, preferred_element_type=jnp.float32)
        * score_scale
    ).astype(jnp.bfloat16)
    key_terms = jnp.einsum(
        "hbij,hbid->hbjd", grad_scores, query_blocks, preferred_element_type=jnp.float32
    )
    grad_key = (fold_keys(key_terms, block_len) * score_scale).astype(jnp.bfloat16)
    return (grad_query, grad_key)


def on_device(queries, key_heads, inputs, cotangent, lengths):
    section_count = lax.axis_size("pipe")
    section_index = lax.axis_index("pipe")
    seq_ways = lax.axis_size("seq")
    tok_rows = queries.shape[1]
    full_width = queries.shape[2]
    head_count = full_width // DH
    kv_count = key_heads.shape[2] // DH
    group_size = head_count // kv_count
    seq_len = tok_rows * seq_ways
    block_count = seq_len // BLK
    local_heads = head_count // seq_ways
    score_scale = DH ** (-0.5)
    last_section = section_count - 1

    seq_index = lax.axis_index("seq")

    def transpose_seq(value, split_axis, concat_axis):
        if seq_ways > 8:
            return lax.all_to_all(value, "seq", split_axis, concat_axis, tiled=True)
        split_size = value.shape[split_axis] // seq_ways
        concat_size = value.shape[concat_axis]
        received = []
        for shift in range(seq_ways):
            target = (seq_index + shift) % seq_ways
            chunk = lax.dynamic_slice_in_dim(value, target * split_size, split_size, axis=split_axis)
            if shift > 0:
                chunk = lax.ppermute(
                    chunk, "seq", [(s, (s + shift) % seq_ways) for s in range(seq_ways)]
                )
            received.append(chunk)
        rising = [received[(seq_ways - k) % seq_ways] for k in range(seq_ways)]
        doubled = jnp.concatenate(rising + rising, axis=concat_axis)
        start = ((seq_ways - seq_index) % seq_ways) * concat_size
        return lax.dynamic_slice_in_dim(doubled, start, seq_ways * concat_size, axis=concat_axis)

    def to_blocks(head_rows):
        return head_rows.reshape(local_heads, block_count, BLK, DH)

    def head_major(rows):
        return jnp.transpose(rows.reshape(tok_rows, head_count, DH), (1, 0, 2))

    stacked = jnp.stack([head_major(queries[0]), head_major(cotangent)])
    stacked_heads = transpose_seq(stacked, 1, 2)
    query_blocks = to_blocks(stacked_heads[0])
    cot_blocks = to_blocks(stacked_heads[1])
    input_heads = transpose_seq(head_major(inputs[0]), 0, 1)
    values_both = key_pair(to_blocks(input_heads))
    kv_pick = (jnp.arange(seq_ways) * local_heads) // group_size
    key_rows = jnp.transpose(key_heads[0].reshape(tok_rows, kv_count, DH), (1, 0, 2))[kv_pick]
    key_flat = lax.all_to_all(key_rows, "seq", split_axis=0, concat_axis=1, tiled=True)
    key_blocks = jnp.broadcast_to(
        key_flat.reshape(1, block_count, BLK, DH), (local_heads, block_count, BLK, DH)
    )
    keys_both = key_pair(key_blocks)
    allowed = visible(lengths, block_count, BLK)
    softmax_probs = probabilities(query_blocks, keys_both, allowed, score_scale)
    probs_low = softmax_probs.astype(jnp.bfloat16)

    grad_ins = []
    grad_outs = []
    grad_in = cot_blocks
    for tick in range(section_count):
        sender = last_section - tick
        new_grad = value_grad(probs_low, grad_in, BLK, seq_ways)
        grad_ins.append(grad_in)
        grad_outs.append(new_grad)
        if sender > 0:
            grad_in = lax.ppermute(new_grad, "pipe", [(sender, sender - 1)])

    def by_section(per_tick):
        chosen = per_tick[0]
        for tick in range(1, section_count):
            chosen = jnp.where(section_index == last_section - tick, per_tick[tick], chosen)
        return chosen

    held_in = by_section(grad_ins)
    held_out = by_section(grad_outs)
    grad_query, grad_key = weight_grads(
        softmax_probs,
        probs_low,
        query_blocks,
        keys_both,
        values_both,
        held_in,
        score_scale,
        BLK,
    )
    pair = jnp.stack([grad_query, held_out]).reshape(2, local_heads, seq_len, DH)
    pair_out = transpose_seq(pair, 2, 1)
    pair_rows = jnp.transpose(pair_out, (0, 2, 1, 3)).reshape(2, tok_rows, full_width)
    if local_heads == 1:
        key_part = grad_key.reshape(seq_len, DH)
    else:
        key_part = jnp.sum(grad_key.astype(jnp.float32), axis=0).reshape(seq_len, DH)
    key_out = lax.all_to_all(key_part[:, None, :], "seq", split_axis=0, concat_axis=1, tiled=True)
    key_sum = jnp.sum(
        key_out.reshape(tok_rows, kv_count, seq_ways // kv_count, DH).astype(jnp.float32), axis=2
    )
    key_final = key_sum.astype(jnp.bfloat16).reshape(tok_rows, kv_count * DH)
    return (pair_rows[0][None], key_final[None], pair_rows[1][None])


def solution(mesh):
    placed = (
        P("pipe", "seq", None),
        P("pipe", "seq", None),
        P("pipe", "seq", None),
        P("seq", None),
        P(),
    )
    return jax.shard_map(
        on_device,
        mesh=mesh,
        in_specs=placed,
        out_specs=(P("pipe", "seq", None), P("pipe", "seq", None), P("pipe", "seq", None)),
        check_vma=False,
    )
```

```python
import jax
import jax.numpy as jnp
from jax import lax
from jax.sharding import PartitionSpec as P

DH = 128
BLK = 128


def key_pair(block_rows):
    first_block = jnp.broadcast_to(block_rows[:, :1], block_rows.shape)
    return jnp.concatenate([first_block, block_rows], axis=2)


def visible(lengths, block_count, block_len):
    shape = (block_count, block_len, 2 * block_len)
    row_index = lax.broadcasted_iota(jnp.int32, shape, 1)
    col_index = lax.broadcasted_iota(jnp.int32, shape, 2)
    block_index = lax.broadcasted_iota(jnp.int32, shape, 0)
    in_first = col_index < block_len
    offset = jnp.where(in_first, col_index, col_index - block_len)
    own_len = lengths[:, None, None]
    first_ok = in_first & (offset < lengths[0]) & ((block_index > 0) | (offset <= row_index))
    own_ok = (
        jnp.logical_not(in_first) & (block_index > 0) & (offset <= row_index) & (offset < own_len)
    )
    return (first_ok | own_ok)[None]


def fold_keys(key_terms, block_len):
    own_part = key_terms[:, :, block_len:]
    first_part = jnp.sum(key_terms[:, :, :block_len], axis=1)
    return own_part.at[:, 0].add(first_part)


def fold_value(key_terms, block_len, groups):
    own_part = key_terms[:, :, block_len:]
    first_terms = key_terms[:, :, :block_len]
    heads, blocks = first_terms.shape[:2]
    grouped = first_terms.reshape((heads, groups, blocks // groups) + first_terms.shape[2:])
    partial_low = lax.optimization_barrier(jnp.sum(grouped, axis=2).astype(jnp.bfloat16))
    first_part = jnp.sum(partial_low.astype(jnp.float32), axis=1)
    return own_part.at[:, 0].add(first_part)


def probabilities(query_blocks, keys_both, allowed, score_scale):
    scores = (
        jnp.einsum("hbid,hbjd->hbij", query_blocks, keys_both, preferred_element_type=jnp.float32)
        * score_scale
    )
    scores = jnp.where(allowed, scores, -jnp.inf)
    row_max = jnp.max(scores, axis=-1, keepdims=True)
    exp_scores = jnp.exp(scores - row_max)
    return exp_scores / jnp.sum(exp_scores, axis=-1, keepdims=True)


def value_grad(probs_low, grad_blocks, block_len, groups):
    key_terms = jnp.einsum(
        "hbij,hbid->hbjd", probs_low, grad_blocks, preferred_element_type=jnp.float32
    )
    return (grad_blocks.astype(jnp.float32) + fold_value(key_terms, block_len, groups)).astype(
        jnp.bfloat16
    )


def weight_grads(
    softmax_probs, probs_low, query_blocks, keys_both, values_both, grad_blocks, score_scale, block_len
):
    output = jnp.einsum(
        "hbij,hbjd->hbid", probs_low, values_both, preferred_element_type=jnp.float32
    )
    row_dot = jnp.sum(grad_blocks.astype(jnp.float32) * output, axis=-1)[..., None]
    grad_probs = jnp.einsum(
        "hbid,hbjd->hbij", grad_blocks, values_both, preferred_element_type=jnp.float32
    )
    grad_scores = (softmax_probs * (grad_probs - row_dot)).astype(jnp.bfloat16)
    grad_query = (
        jnp.einsum("hbij,hbjd->hbid", grad_scores, keys_both, preferred_element_type=jnp.float32)
        * score_scale
    ).astype(jnp.bfloat16)
    key_terms = jnp.einsum(
        "hbij,hbid->hbjd", grad_scores, query_blocks, preferred_element_type=jnp.float32
    )
    grad_key = (fold_keys(key_terms, block_len) * score_scale).astype(jnp.bfloat16)
    return (grad_query, grad_key)


def on_device(queries, key_heads, inputs, cotangent, lengths):
    section_count = lax.axis_size("pipe")
    section_index = lax.axis_index("pipe")
    seq_ways = lax.axis_size("seq")
    tok_rows = queries.shape[1]
    full_width = queries.shape[2]
    head_count = full_width // DH
    kv_count = key_heads.shape[2] // DH
    group_size = head_count // kv_count
    seq_len = tok_rows * seq_ways
    block_count = seq_len // BLK
    local_heads = head_count // seq_ways
    score_scale = DH ** (-0.5)
    last_section = section_count - 1

    seq_index = lax.axis_index("seq")

    def transpose_seq(value, split_axis, concat_axis):
        if seq_ways > 8:
            return lax.all_to_all(value, "seq", split_axis, concat_axis, tiled=True)
        split_size = value.shape[split_axis] // seq_ways
        concat_size = value.shape[concat_axis]
        out_shape = list(value.shape)
        out_shape[split_axis] = split_size
        out_shape[concat_axis] = concat_size * seq_ways
        result = jnp.zeros(out_shape, value.dtype)
        for shift in range(seq_ways):
            target = (seq_index + shift) % seq_ways
            chunk = lax.dynamic_slice_in_dim(value, target * split_size, split_size, axis=split_axis)
            if shift > 0:
                chunk = lax.ppermute(
                    chunk, "seq", [(s, (s + shift) % seq_ways) for s in range(seq_ways)]
                )
            source = (seq_index + seq_ways - shift) % seq_ways
            result = lax.dynamic_update_slice_in_dim(
                result, chunk, source * concat_size, axis=concat_axis
            )
        return result

    def to_blocks(head_rows):
        return head_rows.reshape(local_heads, block_count, BLK, DH)

    def head_major(rows):
        return jnp.transpose(rows.reshape(tok_rows, head_count, DH), (1, 0, 2))

    kv_pick = (jnp.arange(seq_ways) * local_heads) // group_size
    key_rows = jnp.transpose(key_heads[0].reshape(tok_rows, kv_count, DH), (1, 0, 2))[kv_pick]
    per_target = jnp.concatenate(
        [
            head_major(queries[0]).reshape(seq_ways, local_heads, tok_rows, DH),
            head_major(cotangent).reshape(seq_ways, local_heads, tok_rows, DH),
            key_rows.reshape(seq_ways, 1, tok_rows, DH),
        ],
        axis=1,
    ).reshape(seq_ways * (2 * local_heads + 1), tok_rows, DH)
    stacked_heads = transpose_seq(per_target, 0, 1)
    query_blocks = to_blocks(stacked_heads[:local_heads])
    cot_blocks = to_blocks(stacked_heads[local_heads : 2 * local_heads])
    key_flat = stacked_heads[2 * local_heads :]
    input_heads = transpose_seq(head_major(inputs[0]), 0, 1)
    values_both = key_pair(to_blocks(input_heads))
    key_blocks = jnp.broadcast_to(
        key_flat.reshape(1, block_count, BLK, DH), (local_heads, block_count, BLK, DH)
    )
    keys_both = key_pair(key_blocks)
    allowed = visible(lengths, block_count, BLK)
    softmax_probs = probabilities(query_blocks, keys_both, allowed, score_scale)
    probs_low = softmax_probs.astype(jnp.bfloat16)

    grad_ins = []
    grad_outs = []
    grad_in = cot_blocks
    for tick in range(section_count):
        sender = last_section - tick
        new_grad = value_grad(probs_low, grad_in, BLK, seq_ways)
        grad_ins.append(grad_in)
        grad_outs.append(new_grad)
        if sender > 0:
            grad_in = lax.ppermute(new_grad, "pipe", [(sender, sender - 1)])

    def by_section(per_tick):
        chosen = per_tick[0]
        for tick in range(1, section_count):
            chosen = jnp.where(section_index == last_section - tick, per_tick[tick], chosen)
        return chosen

    held_in = by_section(grad_ins)
    held_out = by_section(grad_outs)
    grad_query, grad_key = weight_grads(
        softmax_probs,
        probs_low,
        query_blocks,
        keys_both,
        values_both,
        held_in,
        score_scale,
        BLK,
    )
    if local_heads == 1:
        key_parts = [grad_key.reshape(1, seq_len, DH)]
    else:
        key_sum_local = jnp.sum(grad_key.astype(jnp.float32), axis=0).reshape(seq_len, DH)
        key_high = key_sum_local.astype(jnp.bfloat16)
        key_low = (key_sum_local - key_high.astype(jnp.float32)).astype(jnp.bfloat16)
        key_parts = [key_high[None], key_low[None]]
    key_count = len(key_parts)
    rows_out = jnp.concatenate(
        [grad_query.reshape(local_heads, seq_len, DH), held_out.reshape(local_heads, seq_len, DH)]
        + key_parts,
        axis=0,
    )
    per_source = transpose_seq(rows_out, 1, 0).reshape(
        seq_ways, 2 * local_heads + key_count, tok_rows, DH
    )

    def head_rows(part):
        return jnp.transpose(part.reshape(head_count, tok_rows, DH), (1, 0, 2)).reshape(
            tok_rows, full_width
        )

    query_rows = head_rows(per_source[:, :local_heads])
    grad_rows = head_rows(per_source[:, local_heads : 2 * local_heads])
    key_terms = jnp.sum(per_source[:, 2 * local_heads :].astype(jnp.float32), axis=1)
    key_sum = jnp.sum(key_terms.reshape(kv_count, seq_ways // kv_count, tok_rows, DH), axis=1)
    key_final = (
        jnp.transpose(key_sum, (1, 0, 2)).astype(jnp.bfloat16).reshape(tok_rows, kv_count * DH)
    )
    return (query_rows[None], key_final[None], grad_rows[None])


def solution(mesh):
    placed = (
        P("pipe", "seq", None),
        P("pipe", "seq", None),
        P("pipe", "seq", None),
        P("seq", None),
        P(),
    )
    return jax.shard_map(
        on_device,
        mesh=mesh,
        in_specs=placed,
        out_specs=(P("pipe", "seq", None), P("pipe", "seq", None), P("pipe", "seq", None)),
        check_vma=False,
    )
```

```python
import jax
import jax.numpy as jnp
from jax import lax
from jax.sharding import PartitionSpec as P

DH = 128
BLK = 128


def key_pair(block_rows):
    first_block = jnp.broadcast_to(block_rows[:, :1], block_rows.shape)
    return jnp.concatenate([first_block, block_rows], axis=2)


def visible(lengths, block_count, block_len):
    shape = (block_count, block_len, 2 * block_len)
    row_index = lax.broadcasted_iota(jnp.int32, shape, 1)
    col_index = lax.broadcasted_iota(jnp.int32, shape, 2)
    block_index = lax.broadcasted_iota(jnp.int32, shape, 0)
    in_first = col_index < block_len
    offset = jnp.where(in_first, col_index, col_index - block_len)
    own_len = lengths[:, None, None]
    first_ok = in_first & (offset < lengths[0]) & ((block_index > 0) | (offset <= row_index))
    own_ok = (
        jnp.logical_not(in_first) & (block_index > 0) & (offset <= row_index) & (offset < own_len)
    )
    return (first_ok | own_ok)[None]


def fold_keys(key_terms, block_len):
    own_part = key_terms[:, :, block_len:]
    first_part = jnp.sum(key_terms[:, :, :block_len], axis=1)
    return own_part.at[:, 0].add(first_part)


def fold_value(key_terms, block_len, groups):
    own_part = key_terms[:, :, block_len:]
    first_terms = key_terms[:, :, :block_len]
    heads, blocks = first_terms.shape[:2]
    grouped = first_terms.reshape((heads, groups, blocks // groups) + first_terms.shape[2:])
    partial_low = lax.optimization_barrier(jnp.sum(grouped, axis=2).astype(jnp.bfloat16))
    first_part = jnp.sum(partial_low.astype(jnp.float32), axis=1)
    return own_part.at[:, 0].add(first_part)


def probabilities(query_blocks, keys_both, allowed, score_scale):
    scores = (
        jnp.einsum("hbid,hbjd->hbij", query_blocks, keys_both, preferred_element_type=jnp.float32)
        * score_scale
    )
    scores = jnp.where(allowed, scores, -jnp.inf)
    row_max = jnp.max(scores, axis=-1, keepdims=True)
    exp_scores = jnp.exp(scores - row_max)
    return exp_scores / jnp.sum(exp_scores, axis=-1, keepdims=True)


def value_grad(probs_low, grad_blocks, block_len, groups):
    key_terms = jnp.einsum(
        "hbij,hbid->hbjd", probs_low, grad_blocks, preferred_element_type=jnp.float32
    )
    return (grad_blocks.astype(jnp.float32) + fold_value(key_terms, block_len, groups)).astype(
        jnp.bfloat16
    )


def weight_grads(
    softmax_probs, probs_low, query_blocks, keys_both, values_both, grad_blocks, score_scale, block_len
):
    output = jnp.einsum(
        "hbij,hbjd->hbid", probs_low, values_both, preferred_element_type=jnp.float32
    )
    row_dot = jnp.sum(grad_blocks.astype(jnp.float32) * output, axis=-1)[..., None]
    grad_probs = jnp.einsum(
        "hbid,hbjd->hbij", grad_blocks, values_both, preferred_element_type=jnp.float32
    )
    grad_scores = (softmax_probs * (grad_probs - row_dot)).astype(jnp.bfloat16)
    grad_query = (
        jnp.einsum("hbij,hbjd->hbid", grad_scores, keys_both, preferred_element_type=jnp.float32)
        * score_scale
    ).astype(jnp.bfloat16)
    key_terms = jnp.einsum(
        "hbij,hbid->hbjd", grad_scores, query_blocks, preferred_element_type=jnp.float32
    )
    grad_key = (fold_keys(key_terms, block_len) * score_scale).astype(jnp.bfloat16)
    return (grad_query, grad_key)


def on_device(queries, key_heads, inputs, cotangent, lengths):
    section_count = lax.axis_size("pipe")
    section_index = lax.axis_index("pipe")
    seq_ways = lax.axis_size("seq")
    tok_rows = queries.shape[1]
    full_width = queries.shape[2]
    head_count = full_width // DH
    kv_count = key_heads.shape[2] // DH
    group_size = head_count // kv_count
    seq_len = tok_rows * seq_ways
    block_count = seq_len // BLK
    local_heads = head_count // seq_ways
    score_scale = DH ** (-0.5)
    last_section = section_count - 1

    seq_index = lax.axis_index("seq")

    def transpose_seq(value, split_axis, concat_axis):
        if seq_ways > 8:
            return lax.all_to_all(value, "seq", split_axis, concat_axis, tiled=True)
        split_size = value.shape[split_axis] // seq_ways
        concat_size = value.shape[concat_axis]
        out_shape = list(value.shape)
        out_shape[split_axis] = split_size
        out_shape[concat_axis] = concat_size * seq_ways
        result = jnp.zeros(out_shape, value.dtype)
        for shift in range(seq_ways):
            target = (seq_index + shift) % seq_ways
            chunk = lax.dynamic_slice_in_dim(value, target * split_size, split_size, axis=split_axis)
            if shift > 0:
                chunk = lax.ppermute(
                    chunk, "seq", [(s, (s + shift) % seq_ways) for s in range(seq_ways)]
                )
            source = (seq_index + seq_ways - shift) % seq_ways
            result = lax.dynamic_update_slice_in_dim(
                result, chunk, source * concat_size, axis=concat_axis
            )
        return result

    def to_blocks(head_rows):
        return head_rows.reshape(local_heads, block_count, BLK, DH)

    def head_major(rows):
        return jnp.transpose(rows.reshape(tok_rows, head_count, DH), (1, 0, 2))

    stacked = jnp.stack([head_major(queries[0]), head_major(cotangent), head_major(inputs[0])])
    stacked_heads = transpose_seq(stacked, 1, 2)
    query_blocks = to_blocks(stacked_heads[0])
    cot_blocks = to_blocks(stacked_heads[1])
    values_both = key_pair(to_blocks(stacked_heads[2]))
    kv_pick = (jnp.arange(seq_ways) * local_heads) // group_size
    key_rows = jnp.transpose(key_heads[0].reshape(tok_rows, kv_count, DH), (1, 0, 2))[kv_pick]
    key_flat = lax.all_to_all(key_rows, "seq", split_axis=0, concat_axis=1, tiled=True)
    key_blocks = jnp.broadcast_to(
        key_flat.reshape(1, block_count, BLK, DH), (local_heads, block_count, BLK, DH)
    )
    keys_both = key_pair(key_blocks)
    allowed = visible(lengths, block_count, BLK)
    softmax_probs = probabilities(query_blocks, keys_both, allowed, score_scale)
    probs_low = softmax_probs.astype(jnp.bfloat16)

    grad_ins = []
    grad_outs = []
    grad_in = cot_blocks
    for tick in range(section_count):
        sender = last_section - tick
        new_grad = value_grad(probs_low, grad_in, BLK, seq_ways)
        grad_ins.append(grad_in)
        grad_outs.append(new_grad)
        if sender > 0:
            grad_in = lax.ppermute(new_grad, "pipe", [(sender, sender - 1)])

    def by_section(per_tick):
        chosen = per_tick[0]
        for tick in range(1, section_count):
            chosen = jnp.where(section_index == last_section - tick, per_tick[tick], chosen)
        return chosen

    held_in = by_section(grad_ins)
    held_out = by_section(grad_outs)
    grad_query, grad_key = weight_grads(
        softmax_probs,
        probs_low,
        query_blocks,
        keys_both,
        values_both,
        held_in,
        score_scale,
        BLK,
    )
    pair = jnp.stack([grad_query, held_out]).reshape(2, local_heads, seq_len, DH)
    pair_out = transpose_seq(pair, 2, 1)
    pair_rows = jnp.transpose(pair_out, (0, 2, 1, 3)).reshape(2, tok_rows, full_width)
    if local_heads == 1:
        key_part = grad_key.reshape(seq_len, DH)
    else:
        key_part = jnp.sum(grad_key.astype(jnp.float32), axis=0).reshape(seq_len, DH)
    key_out = lax.all_to_all(key_part[:, None, :], "seq", split_axis=0, concat_axis=1, tiled=True)
    key_sum = jnp.sum(
        key_out.reshape(tok_rows, kv_count, seq_ways // kv_count, DH).astype(jnp.float32), axis=2
    )
    key_final = key_sum.astype(jnp.bfloat16).reshape(tok_rows, kv_count * DH)
    return (pair_rows[0][None], key_final[None], pair_rows[1][None])


def solution(mesh):
    placed = (
        P("pipe", "seq", None),
        P("pipe", "seq", None),
        P("pipe", "seq", None),
        P("seq", None),
        P(),
    )
    return jax.shard_map(
        on_device,
        mesh=mesh,
        in_specs=placed,
        out_specs=(P("pipe", "seq", None), P("pipe", "seq", None), P("pipe", "seq", None)),
        check_vma=False,
    )
```

```python
import jax
import jax.numpy as jnp
from jax import lax
from jax.sharding import PartitionSpec as P

DH = 128
BLK = 128


def key_pair(block_rows):
    first_block = jnp.broadcast_to(block_rows[:, :1], block_rows.shape)
    return jnp.concatenate([first_block, block_rows], axis=2)


def visible(lengths, block_count, block_len):
    shape = (block_count, block_len, 2 * block_len)
    row_index = lax.broadcasted_iota(jnp.int32, shape, 1)
    col_index = lax.broadcasted_iota(jnp.int32, shape, 2)
    block_index = lax.broadcasted_iota(jnp.int32, shape, 0)
    in_first = col_index < block_len
    offset = jnp.where(in_first, col_index, col_index - block_len)
    own_len = lengths[:, None, None]
    first_ok = in_first & (offset < lengths[0]) & ((block_index > 0) | (offset <= row_index))
    own_ok = (
        jnp.logical_not(in_first) & (block_index > 0) & (offset <= row_index) & (offset < own_len)
    )
    return (first_ok | own_ok)[None]


def fold_keys(key_terms, block_len):
    own_part = key_terms[:, :, block_len:]
    first_part = jnp.sum(key_terms[:, :, :block_len], axis=1)
    return own_part.at[:, 0].add(first_part)


def fold_value(key_terms, block_len, groups):
    own_part = key_terms[:, :, block_len:]
    first_terms = key_terms[:, :, :block_len]
    heads, blocks = first_terms.shape[:2]
    grouped = first_terms.reshape((heads, groups, blocks // groups) + first_terms.shape[2:])
    partial_low = lax.optimization_barrier(jnp.sum(grouped, axis=2).astype(jnp.bfloat16))
    first_part = jnp.sum(partial_low.astype(jnp.float32), axis=1)
    return own_part.at[:, 0].add(first_part)


def probabilities(query_blocks, keys_both, allowed, score_scale):
    scores = (
        jnp.einsum("hbid,hbjd->hbij", query_blocks, keys_both, preferred_element_type=jnp.float32)
        * score_scale
    )
    scores = jnp.where(allowed, scores, -jnp.inf)
    row_max = jnp.max(scores, axis=-1, keepdims=True)
    exp_scores = jnp.exp(scores - row_max)
    return exp_scores / jnp.sum(exp_scores, axis=-1, keepdims=True)


def value_grad(probs_low, grad_blocks, block_len, groups):
    key_terms = jnp.einsum(
        "hbij,hbid->hbjd", probs_low, grad_blocks, preferred_element_type=jnp.float32
    )
    return (grad_blocks.astype(jnp.float32) + fold_value(key_terms, block_len, groups)).astype(
        jnp.bfloat16
    )


def weight_grads(
    softmax_probs, probs_low, query_blocks, keys_both, values_both, grad_blocks, score_scale, block_len
):
    output = jnp.einsum(
        "hbij,hbjd->hbid", probs_low, values_both, preferred_element_type=jnp.float32
    )
    row_dot = jnp.sum(grad_blocks.astype(jnp.float32) * output, axis=-1)[..., None]
    grad_probs = jnp.einsum(
        "hbid,hbjd->hbij", grad_blocks, values_both, preferred_element_type=jnp.float32
    )
    grad_scores = (softmax_probs * (grad_probs - row_dot)).astype(jnp.bfloat16)
    grad_query = (
        jnp.einsum("hbij,hbjd->hbid", grad_scores, keys_both, preferred_element_type=jnp.float32)
        * score_scale
    ).astype(jnp.bfloat16)
    key_terms = jnp.einsum(
        "hbij,hbid->hbjd", grad_scores, query_blocks, preferred_element_type=jnp.float32
    )
    grad_key = (fold_keys(key_terms, block_len) * score_scale).astype(jnp.bfloat16)
    return (grad_query, grad_key)


def on_device(queries, key_heads, inputs, cotangent, lengths):
    section_count = lax.axis_size("pipe")
    section_index = lax.axis_index("pipe")
    seq_ways = lax.axis_size("seq")
    tok_rows = queries.shape[1]
    full_width = queries.shape[2]
    head_count = full_width // DH
    kv_count = key_heads.shape[2] // DH
    group_size = head_count // kv_count
    seq_len = tok_rows * seq_ways
    block_count = seq_len // BLK
    local_heads = head_count // seq_ways
    score_scale = DH ** (-0.5)
    last_section = section_count - 1

    seq_index = lax.axis_index("seq")

    def transpose_seq(value, split_axis, concat_axis):
        if seq_ways > 8:
            return lax.all_to_all(value, "seq", split_axis, concat_axis, tiled=True)
        split_size = value.shape[split_axis] // seq_ways
        concat_size = value.shape[concat_axis]
        out_shape = list(value.shape)
        out_shape[split_axis] = split_size
        out_shape[concat_axis] = concat_size * seq_ways
        result = jnp.zeros(out_shape, value.dtype)
        for shift in range(seq_ways):
            target = (seq_index + shift) % seq_ways
            chunk = lax.dynamic_slice_in_dim(value, target * split_size, split_size, axis=split_axis)
            if shift > 0:
                chunk = lax.ppermute(
                    chunk, "seq", [(s, (s + shift) % seq_ways) for s in range(seq_ways)]
                )
            source = (seq_index + seq_ways - shift) % seq_ways
            result = lax.dynamic_update_slice_in_dim(
                result, chunk, source * concat_size, axis=concat_axis
            )
        return result

    def to_blocks(head_rows):
        return head_rows.reshape(local_heads, block_count, BLK, DH)

    def head_major(rows):
        return jnp.transpose(rows.reshape(tok_rows, head_count, DH), (1, 0, 2))

    kv_pick = (jnp.arange(seq_ways) * local_heads) // group_size
    key_rows = jnp.transpose(key_heads[0].reshape(tok_rows, kv_count, DH), (1, 0, 2))[kv_pick]
    per_target = jnp.concatenate(
        [
            head_major(queries[0]).reshape(seq_ways, local_heads, tok_rows, DH),
            head_major(cotangent).reshape(seq_ways, local_heads, tok_rows, DH),
            key_rows.reshape(seq_ways, 1, tok_rows, DH),
        ],
        axis=1,
    ).reshape(seq_ways * (2 * local_heads + 1), tok_rows, DH)
    stacked_heads = transpose_seq(per_target, 0, 1)
    query_blocks = to_blocks(stacked_heads[:local_heads])
    cot_blocks = to_blocks(stacked_heads[local_heads : 2 * local_heads])
    key_flat = stacked_heads[2 * local_heads :]
    input_heads = transpose_seq(head_major(inputs[0]), 0, 1)
    values_both = key_pair(to_blocks(input_heads))
    key_blocks = jnp.broadcast_to(
        key_flat.reshape(1, block_count, BLK, DH), (local_heads, block_count, BLK, DH)
    )
    keys_both = key_pair(key_blocks)
    allowed = visible(lengths, block_count, BLK)
    softmax_probs = probabilities(query_blocks, keys_both, allowed, score_scale)
    probs_low = softmax_probs.astype(jnp.bfloat16)

    grad_ins = []
    grad_outs = []
    grad_in = cot_blocks
    for tick in range(section_count):
        sender = last_section - tick
        new_grad = value_grad(probs_low, grad_in, BLK, seq_ways)
        grad_ins.append(grad_in)
        grad_outs.append(new_grad)
        if sender > 0:
            grad_in = lax.ppermute(new_grad, "pipe", [(sender, sender - 1)])

    def by_section(per_tick):
        chosen = per_tick[0]
        for tick in range(1, section_count):
            chosen = jnp.where(section_index == last_section - tick, per_tick[tick], chosen)
        return chosen

    held_in = by_section(grad_ins)
    held_out = by_section(grad_outs)
    grad_query, grad_key = weight_grads(
        softmax_probs,
        probs_low,
        query_blocks,
        keys_both,
        values_both,
        held_in,
        score_scale,
        BLK,
    )
    pair = jnp.stack([grad_query, held_out]).reshape(2, local_heads, seq_len, DH)
    pair_out = transpose_seq(pair, 2, 1)
    pair_rows = jnp.transpose(pair_out, (0, 2, 1, 3)).reshape(2, tok_rows, full_width)
    if local_heads == 1:
        key_part = grad_key.reshape(seq_len, DH)
    else:
        key_part = jnp.sum(grad_key.astype(jnp.float32), axis=0).reshape(seq_len, DH)
    key_out = lax.all_to_all(key_part[:, None, :], "seq", split_axis=0, concat_axis=1, tiled=True)
    key_sum = jnp.sum(
        key_out.reshape(tok_rows, kv_count, seq_ways // kv_count, DH).astype(jnp.float32), axis=2
    )
    key_final = key_sum.astype(jnp.bfloat16).reshape(tok_rows, kv_count * DH)
    return (pair_rows[0][None], key_final[None], pair_rows[1][None])


def solution(mesh):
    placed = (
        P("pipe", "seq", None),
        P("pipe", "seq", None),
        P("pipe", "seq", None),
        P("seq", None),
        P(),
    )
    return jax.shard_map(
        on_device,
        mesh=mesh,
        in_specs=placed,
        out_specs=(P("pipe", "seq", None), P("pipe", "seq", None), P("pipe", "seq", None)),
        check_vma=False,
    )
```

```python
import jax
import jax.numpy as jnp
from jax import lax
from jax.sharding import PartitionSpec as P

DH = 128
BLK = 128


def key_pair(block_rows):
    first_block = jnp.broadcast_to(block_rows[:, :1], block_rows.shape)
    return jnp.concatenate([first_block, block_rows], axis=2)


def visible(lengths, block_count, block_len):
    shape = (block_count, block_len, 2 * block_len)
    row_index = lax.broadcasted_iota(jnp.int32, shape, 1)
    col_index = lax.broadcasted_iota(jnp.int32, shape, 2)
    block_index = lax.broadcasted_iota(jnp.int32, shape, 0)
    in_first = col_index < block_len
    offset = jnp.where(in_first, col_index, col_index - block_len)
    own_len = lengths[:, None, None]
    first_ok = in_first & (offset < lengths[0]) & ((block_index > 0) | (offset <= row_index))
    own_ok = (
        jnp.logical_not(in_first) & (block_index > 0) & (offset <= row_index) & (offset < own_len)
    )
    return (first_ok | own_ok)[None]


def fold_keys(key_terms, block_len):
    own_part = key_terms[:, :, block_len:]
    first_part = jnp.sum(key_terms[:, :, :block_len], axis=1)
    return own_part.at[:, 0].add(first_part)


def fold_value(key_terms, block_len, groups):
    own_part = key_terms[:, :, block_len:]
    first_terms = key_terms[:, :, :block_len]
    heads, blocks = first_terms.shape[:2]
    grouped = first_terms.reshape((heads, groups, blocks // groups) + first_terms.shape[2:])
    partial_low = lax.optimization_barrier(jnp.sum(grouped, axis=2).astype(jnp.bfloat16))
    first_part = jnp.sum(partial_low.astype(jnp.float32), axis=1)
    return own_part.at[:, 0].add(first_part)


def probabilities(query_blocks, keys_both, allowed, score_scale):
    scores = (
        jnp.einsum("hbid,hbjd->hbij", query_blocks, keys_both, preferred_element_type=jnp.float32)
        * score_scale
    )
    scores = jnp.where(allowed, scores, -jnp.inf)
    row_max = jnp.max(scores, axis=-1, keepdims=True)
    exp_scores = jnp.exp(scores - row_max)
    return exp_scores / jnp.sum(exp_scores, axis=-1, keepdims=True)


def value_grad(probs_low, grad_blocks, block_len, groups):
    key_terms = jnp.einsum(
        "hbij,hbid->hbjd", probs_low, grad_blocks, preferred_element_type=jnp.float32
    )
    return (grad_blocks.astype(jnp.float32) + fold_value(key_terms, block_len, groups)).astype(
        jnp.bfloat16
    )


def weight_grads(
    softmax_probs, probs_low, query_blocks, keys_both, values_both, grad_blocks, score_scale, block_len
):
    output = jnp.einsum(
        "hbij,hbjd->hbid", probs_low, values_both, preferred_element_type=jnp.float32
    )
    row_dot = jnp.sum(grad_blocks.astype(jnp.float32) * output, axis=-1)[..., None]
    grad_probs = jnp.einsum(
        "hbid,hbjd->hbij", grad_blocks, values_both, preferred_element_type=jnp.float32
    )
    grad_scores = (softmax_probs * (grad_probs - row_dot)).astype(jnp.bfloat16)
    grad_query = (
        jnp.einsum("hbij,hbjd->hbid", grad_scores, keys_both, preferred_element_type=jnp.float32)
        * score_scale
    ).astype(jnp.bfloat16)
    key_terms = jnp.einsum(
        "hbij,hbid->hbjd", grad_scores, query_blocks, preferred_element_type=jnp.float32
    )
    grad_key = (fold_keys(key_terms, block_len) * score_scale).astype(jnp.bfloat16)
    return (grad_query, grad_key)


def on_device(queries, key_heads, inputs, cotangent, lengths):
    section_count = lax.axis_size("pipe")
    section_index = lax.axis_index("pipe")
    seq_ways = lax.axis_size("seq")
    tok_rows = queries.shape[1]
    full_width = queries.shape[2]
    head_count = full_width // DH
    kv_count = key_heads.shape[2] // DH
    group_size = head_count // kv_count
    seq_len = tok_rows * seq_ways
    block_count = seq_len // BLK
    local_heads = head_count // seq_ways
    score_scale = DH ** (-0.5)
    last_section = section_count - 1

    seq_index = lax.axis_index("seq")

    def transpose_seq(value, split_axis, concat_axis, section=None):
        if seq_ways > 8:
            return lax.all_to_all(value, "seq", split_axis, concat_axis, tiled=True)
        split_size = value.shape[split_axis] // seq_ways
        concat_size = value.shape[concat_axis]
        out_shape = list(value.shape)
        out_shape[split_axis] = split_size
        out_shape[concat_axis] = concat_size * seq_ways
        result = jnp.zeros(out_shape, value.dtype)
        for shift in range(seq_ways):
            target = (seq_index + shift) % seq_ways
            chunk = lax.dynamic_slice_in_dim(value, target * split_size, split_size, axis=split_axis)
            if shift > 0 and section is None:
                chunk = lax.ppermute(
                    chunk, "seq", [(s, (s + shift) % seq_ways) for s in range(seq_ways)]
                )
            elif shift > 0:
                base = section * seq_ways
                chunk = lax.ppermute(
                    chunk,
                    ("pipe", "seq"),
                    [(base + s, base + (s + shift) % seq_ways) for s in range(seq_ways)],
                )
            source = (seq_index + seq_ways - shift) % seq_ways
            result = lax.dynamic_update_slice_in_dim(
                result, chunk, source * concat_size, axis=concat_axis
            )
        return result

    def to_blocks(head_rows):
        return head_rows.reshape(local_heads, block_count, BLK, DH)

    def head_major(rows):
        return jnp.transpose(rows.reshape(tok_rows, head_count, DH), (1, 0, 2))

    is_last = section_index == last_section
    second = jnp.where(is_last, head_major(cotangent), head_major(inputs[0]))
    stacked = jnp.stack([head_major(queries[0]), second])
    stacked_heads = transpose_seq(stacked, 1, 2)
    query_blocks = to_blocks(stacked_heads[0])
    cot_blocks = to_blocks(stacked_heads[1])
    last_inputs = transpose_seq(head_major(inputs[0]), 0, 1, section=last_section)
    input_heads = jnp.where(is_last, last_inputs, stacked_heads[1])
    values_both = key_pair(to_blocks(input_heads))
    kv_pick = (jnp.arange(seq_ways) * local_heads) // group_size
    key_rows = jnp.transpose(key_heads[0].reshape(tok_rows, kv_count, DH), (1, 0, 2))[kv_pick]
    key_flat = lax.all_to_all(key_rows, "seq", split_axis=0, concat_axis=1, tiled=True)
    key_blocks = jnp.broadcast_to(
        key_flat.reshape(1, block_count, BLK, DH), (local_heads, block_count, BLK, DH)
    )
    keys_both = key_pair(key_blocks)
    allowed = visible(lengths, block_count, BLK)
    softmax_probs = probabilities(query_blocks, keys_both, allowed, score_scale)
    probs_low = softmax_probs.astype(jnp.bfloat16)

    grad_ins = []
    grad_outs = []
    grad_in = cot_blocks
    for tick in range(section_count):
        sender = last_section - tick
        new_grad = value_grad(probs_low, grad_in, BLK, seq_ways)
        grad_ins.append(grad_in)
        grad_outs.append(new_grad)
        if sender > 0:
            grad_in = lax.ppermute(new_grad, "pipe", [(sender, sender - 1)])

    def by_section(per_tick):
        chosen = per_tick[0]
        for tick in range(1, section_count):
            chosen = jnp.where(section_index == last_section - tick, per_tick[tick], chosen)
        return chosen

    held_in = by_section(grad_ins)
    held_out = by_section(grad_outs)
    grad_query, grad_key = weight_grads(
        softmax_probs,
        probs_low,
        query_blocks,
        keys_both,
        values_both,
        held_in,
        score_scale,
        BLK,
    )
    pair = jnp.stack([grad_query, held_out]).reshape(2, local_heads, seq_len, DH)
    pair_out = transpose_seq(pair, 2, 1)
    pair_rows = jnp.transpose(pair_out, (0, 2, 1, 3)).reshape(2, tok_rows, full_width)
    if local_heads == 1:
        key_part = grad_key.reshape(seq_len, DH)
    else:
        key_part = jnp.sum(grad_key.astype(jnp.float32), axis=0).reshape(seq_len, DH)
    key_out = lax.all_to_all(key_part[:, None, :], "seq", split_axis=0, concat_axis=1, tiled=True)
    key_sum = jnp.sum(
        key_out.reshape(tok_rows, kv_count, seq_ways // kv_count, DH).astype(jnp.float32), axis=2
    )
    key_final = key_sum.astype(jnp.bfloat16).reshape(tok_rows, kv_count * DH)
    return (pair_rows[0][None], key_final[None], pair_rows[1][None])


def solution(mesh):
    placed = (
        P("pipe", "seq", None),
        P("pipe", "seq", None),
        P("pipe", "seq", None),
        P("seq", None),
        P(),
    )
    return jax.shard_map(
        on_device,
        mesh=mesh,
        in_specs=placed,
        out_specs=(P("pipe", "seq", None), P("pipe", "seq", None), P("pipe", "seq", None)),
        check_vma=False,
    )
```

```python
import jax
import jax.numpy as jnp
from jax import lax
from jax.sharding import PartitionSpec as P

DH = 128
BLK = 128


def key_pair(block_rows):
    first_block = jnp.broadcast_to(block_rows[:, :1], block_rows.shape)
    return jnp.concatenate([first_block, block_rows], axis=2)


def visible(lengths, block_count, block_len):
    shape = (block_count, block_len, 2 * block_len)
    row_index = lax.broadcasted_iota(jnp.int32, shape, 1)
    col_index = lax.broadcasted_iota(jnp.int32, shape, 2)
    block_index = lax.broadcasted_iota(jnp.int32, shape, 0)
    in_first = col_index < block_len
    offset = jnp.where(in_first, col_index, col_index - block_len)
    own_len = lengths[:, None, None]
    first_ok = in_first & (offset < lengths[0]) & ((block_index > 0) | (offset <= row_index))
    own_ok = (
        jnp.logical_not(in_first) & (block_index > 0) & (offset <= row_index) & (offset < own_len)
    )
    return (first_ok | own_ok)[None]


def fold_keys(key_terms, block_len):
    own_part = key_terms[:, :, block_len:]
    first_part = jnp.sum(key_terms[:, :, :block_len], axis=1)
    return own_part.at[:, 0].add(first_part)


def fold_value(key_terms, block_len, groups):
    own_part = key_terms[:, :, block_len:]
    first_terms = key_terms[:, :, :block_len]
    heads, blocks = first_terms.shape[:2]
    grouped = first_terms.reshape((heads, groups, blocks // groups) + first_terms.shape[2:])
    partial_low = lax.optimization_barrier(jnp.sum(grouped, axis=2).astype(jnp.bfloat16))
    first_part = jnp.sum(partial_low.astype(jnp.float32), axis=1)
    return own_part.at[:, 0].add(first_part)


def probabilities(query_blocks, keys_both, allowed, score_scale):
    scores = (
        jnp.einsum("hbid,hbjd->hbij", query_blocks, keys_both, preferred_element_type=jnp.float32)
        * score_scale
    )
    scores = jnp.where(allowed, scores, -jnp.inf)
    row_max = jnp.max(scores, axis=-1, keepdims=True)
    exp_scores = jnp.exp(scores - row_max)
    return exp_scores / jnp.sum(exp_scores, axis=-1, keepdims=True)


def value_grad(probs_low, grad_blocks, block_len, groups):
    key_terms = jnp.einsum(
        "hbij,hbid->hbjd", probs_low, grad_blocks, preferred_element_type=jnp.float32
    )
    return (grad_blocks.astype(jnp.float32) + fold_value(key_terms, block_len, groups)).astype(
        jnp.bfloat16
    )


def weight_grads(
    softmax_probs, probs_low, query_blocks, keys_both, values_both, grad_blocks, score_scale, block_len
):
    output = jnp.einsum(
        "hbij,hbjd->hbid", probs_low, values_both, preferred_element_type=jnp.float32
    )
    row_dot = jnp.sum(grad_blocks.astype(jnp.float32) * output, axis=-1)[..., None]
    grad_probs = jnp.einsum(
        "hbid,hbjd->hbij", grad_blocks, values_both, preferred_element_type=jnp.float32
    )
    grad_scores = (softmax_probs * (grad_probs - row_dot)).astype(jnp.bfloat16)
    grad_query = (
        jnp.einsum("hbij,hbjd->hbid", grad_scores, keys_both, preferred_element_type=jnp.float32)
        * score_scale
    ).astype(jnp.bfloat16)
    key_terms = jnp.einsum(
        "hbij,hbid->hbjd", grad_scores, query_blocks, preferred_element_type=jnp.float32
    )
    grad_key = (fold_keys(key_terms, block_len) * score_scale).astype(jnp.bfloat16)
    return (grad_query, grad_key)


def on_device(queries, key_heads, inputs, cotangent, lengths):
    section_count = lax.axis_size("pipe")
    section_index = lax.axis_index("pipe")
    seq_ways = lax.axis_size("seq")
    tok_rows = queries.shape[1]
    full_width = queries.shape[2]
    head_count = full_width // DH
    kv_count = key_heads.shape[2] // DH
    group_size = head_count // kv_count
    seq_len = tok_rows * seq_ways
    block_count = seq_len // BLK
    local_heads = head_count // seq_ways
    score_scale = DH ** (-0.5)
    last_section = section_count - 1

    seq_index = lax.axis_index("seq")

    def transpose_seq(value, split_axis, concat_axis, section=None):
        if seq_ways > 8:
            return lax.all_to_all(value, "seq", split_axis, concat_axis, tiled=True)
        split_size = value.shape[split_axis] // seq_ways
        concat_size = value.shape[concat_axis]
        out_shape = list(value.shape)
        out_shape[split_axis] = split_size
        out_shape[concat_axis] = concat_size * seq_ways
        received = []
        for shift in range(seq_ways):
            target = (seq_index + shift) % seq_ways
            chunk = lax.dynamic_slice_in_dim(value, target * split_size, split_size, axis=split_axis)
            if shift > 0 and section is None:
                chunk = lax.ppermute(
                    chunk, "seq", [(s, (s + shift) % seq_ways) for s in range(seq_ways)]
                )
            elif shift > 0:
                base = section * seq_ways
                chunk = lax.ppermute(
                    chunk,
                    ("pipe", "seq"),
                    [(base + s, base + (s + shift) % seq_ways) for s in range(seq_ways)],
                )
            received.append(chunk)

        def assemble(chunks):
            result = jnp.zeros(out_shape, value.dtype)
            for shift, chunk in enumerate(chunks):
                source = (seq_index + seq_ways - shift) % seq_ways
                result = lax.dynamic_update_slice_in_dim(
                    result, chunk, source * concat_size, axis=concat_axis
                )
            return result

        if section is None:
            return assemble(received)
        return lax.cond(
            section_index == section,
            assemble,
            lambda chunks: jnp.zeros(out_shape, value.dtype),
            received,
        )

    def to_blocks(head_rows):
        return head_rows.reshape(local_heads, block_count, BLK, DH)

    def head_major(rows):
        return jnp.transpose(rows.reshape(tok_rows, head_count, DH), (1, 0, 2))

    is_last = section_index == last_section
    second = jnp.where(is_last, head_major(cotangent), head_major(inputs[0]))
    stacked = jnp.stack([head_major(queries[0]), second])
    stacked_heads = transpose_seq(stacked, 1, 2)
    query_blocks = to_blocks(stacked_heads[0])
    cot_blocks = to_blocks(stacked_heads[1])
    last_inputs = transpose_seq(head_major(inputs[0]), 0, 1, section=last_section)
    input_heads = jnp.where(is_last, last_inputs, stacked_heads[1])
    values_both = key_pair(to_blocks(input_heads))
    kv_pick = (jnp.arange(seq_ways) * local_heads) // group_size
    key_rows = jnp.transpose(key_heads[0].reshape(tok_rows, kv_count, DH), (1, 0, 2))[kv_pick]
    key_flat = lax.all_to_all(key_rows, "seq", split_axis=0, concat_axis=1, tiled=True)
    key_blocks = jnp.broadcast_to(
        key_flat.reshape(1, block_count, BLK, DH), (local_heads, block_count, BLK, DH)
    )
    keys_both = key_pair(key_blocks)
    allowed = visible(lengths, block_count, BLK)
    softmax_probs = probabilities(query_blocks, keys_both, allowed, score_scale)
    probs_low = softmax_probs.astype(jnp.bfloat16)

    grad_ins = []
    grad_outs = []
    grad_in = cot_blocks
    for tick in range(section_count):
        sender = last_section - tick
        new_grad = value_grad(probs_low, grad_in, BLK, seq_ways)
        grad_ins.append(grad_in)
        grad_outs.append(new_grad)
        if sender > 0:
            grad_in = lax.ppermute(new_grad, "pipe", [(sender, sender - 1)])

    def by_section(per_tick):
        chosen = per_tick[0]
        for tick in range(1, section_count):
            chosen = jnp.where(section_index == last_section - tick, per_tick[tick], chosen)
        return chosen

    held_in = by_section(grad_ins)
    held_out = by_section(grad_outs)
    grad_query, grad_key = weight_grads(
        softmax_probs,
        probs_low,
        query_blocks,
        keys_both,
        values_both,
        held_in,
        score_scale,
        BLK,
    )
    pair = jnp.stack([grad_query, held_out]).reshape(2, local_heads, seq_len, DH)
    pair_out = transpose_seq(pair, 2, 1)
    pair_rows = jnp.transpose(pair_out, (0, 2, 1, 3)).reshape(2, tok_rows, full_width)
    if local_heads == 1:
        key_part = grad_key.reshape(seq_len, DH)
    else:
        key_part = jnp.sum(grad_key.astype(jnp.float32), axis=0).reshape(seq_len, DH)
    key_out = lax.all_to_all(key_part[:, None, :], "seq", split_axis=0, concat_axis=1, tiled=True)
    key_sum = jnp.sum(
        key_out.reshape(tok_rows, kv_count, seq_ways // kv_count, DH).astype(jnp.float32), axis=2
    )
    key_final = key_sum.astype(jnp.bfloat16).reshape(tok_rows, kv_count * DH)
    return (pair_rows[0][None], key_final[None], pair_rows[1][None])


def solution(mesh):
    placed = (
        P("pipe", "seq", None),
        P("pipe", "seq", None),
        P("pipe", "seq", None),
        P("seq", None),
        P(),
    )
    return jax.shard_map(
        on_device,
        mesh=mesh,
        in_specs=placed,
        out_specs=(P("pipe", "seq", None), P("pipe", "seq", None), P("pipe", "seq", None)),
        check_vma=False,
    )
```

```python
import jax
import jax.numpy as jnp
from jax import lax
from jax.sharding import PartitionSpec as P

DH = 128
BLK = 128


def key_pair(block_rows):
    first_block = jnp.broadcast_to(block_rows[:, :1], block_rows.shape)
    return jnp.concatenate([first_block, block_rows], axis=2)


def visible(lengths, block_count, block_len):
    shape = (block_count, block_len, 2 * block_len)
    row_index = lax.broadcasted_iota(jnp.int32, shape, 1)
    col_index = lax.broadcasted_iota(jnp.int32, shape, 2)
    block_index = lax.broadcasted_iota(jnp.int32, shape, 0)
    in_first = col_index < block_len
    offset = jnp.where(in_first, col_index, col_index - block_len)
    own_len = lengths[:, None, None]
    first_ok = in_first & (offset < lengths[0]) & ((block_index > 0) | (offset <= row_index))
    own_ok = (
        jnp.logical_not(in_first) & (block_index > 0) & (offset <= row_index) & (offset < own_len)
    )
    return (first_ok | own_ok)[None]


def fold_keys(key_terms, block_len):
    own_part = key_terms[:, :, block_len:]
    first_part = jnp.sum(key_terms[:, :, :block_len], axis=1)
    return own_part.at[:, 0].add(first_part)


def fold_value(key_terms, block_len, groups):
    own_part = key_terms[:, :, block_len:]
    first_terms = key_terms[:, :, :block_len]
    heads, blocks = first_terms.shape[:2]
    grouped = first_terms.reshape((heads, groups, blocks // groups) + first_terms.shape[2:])
    partial_low = lax.optimization_barrier(jnp.sum(grouped, axis=2).astype(jnp.bfloat16))
    first_part = jnp.sum(partial_low.astype(jnp.float32), axis=1)
    return own_part.at[:, 0].add(first_part)


def probabilities(query_blocks, keys_both, allowed, score_scale):
    scores = (
        jnp.einsum("hbid,hbjd->hbij", query_blocks, keys_both, preferred_element_type=jnp.float32)
        * score_scale
    )
    scores = jnp.where(allowed, scores, -jnp.inf)
    row_max = jnp.max(scores, axis=-1, keepdims=True)
    exp_scores = jnp.exp(scores - row_max)
    return exp_scores / jnp.sum(exp_scores, axis=-1, keepdims=True)


def value_grad(probs_low, grad_blocks, block_len, groups):
    key_terms = jnp.einsum(
        "hbij,hbid->hbjd", probs_low, grad_blocks, preferred_element_type=jnp.float32
    )
    return (grad_blocks.astype(jnp.float32) + fold_value(key_terms, block_len, groups)).astype(
        jnp.bfloat16
    )


def weight_grads(
    softmax_probs, probs_low, query_blocks, keys_both, values_both, grad_blocks, score_scale, block_len
):
    output = jnp.einsum(
        "hbij,hbjd->hbid", probs_low, values_both, preferred_element_type=jnp.float32
    )
    row_dot = jnp.sum(grad_blocks.astype(jnp.float32) * output, axis=-1)[..., None]
    grad_probs = jnp.einsum(
        "hbid,hbjd->hbij", grad_blocks, values_both, preferred_element_type=jnp.float32
    )
    grad_scores = (softmax_probs * (grad_probs - row_dot)).astype(jnp.bfloat16)
    grad_query = (
        jnp.einsum("hbij,hbjd->hbid", grad_scores, keys_both, preferred_element_type=jnp.float32)
        * score_scale
    ).astype(jnp.bfloat16)
    key_terms = jnp.einsum(
        "hbij,hbid->hbjd", grad_scores, query_blocks, preferred_element_type=jnp.float32
    )
    grad_key = (fold_keys(key_terms, block_len) * score_scale).astype(jnp.bfloat16)
    return (grad_query, grad_key)


def on_device(queries, key_heads, inputs, cotangent, lengths):
    section_count = lax.axis_size("pipe")
    section_index = lax.axis_index("pipe")
    seq_ways = lax.axis_size("seq")
    tok_rows = queries.shape[1]
    full_width = queries.shape[2]
    head_count = full_width // DH
    kv_count = key_heads.shape[2] // DH
    group_size = head_count // kv_count
    seq_len = tok_rows * seq_ways
    block_count = seq_len // BLK
    local_heads = head_count // seq_ways
    score_scale = DH ** (-0.5)
    last_section = section_count - 1

    seq_index = lax.axis_index("seq")

    def transpose_seq(value, split_axis, concat_axis, section=None):
        if seq_ways > 8:
            return lax.all_to_all(value, "seq", split_axis, concat_axis, tiled=True)
        split_size = value.shape[split_axis] // seq_ways
        concat_size = value.shape[concat_axis]
        out_shape = list(value.shape)
        out_shape[split_axis] = split_size
        out_shape[concat_axis] = concat_size * seq_ways
        result = jnp.zeros(out_shape, value.dtype)
        for shift in range(seq_ways):
            target = (seq_index + shift) % seq_ways
            chunk = lax.dynamic_slice_in_dim(value, target * split_size, split_size, axis=split_axis)
            if shift > 0 and section is None:
                chunk = lax.ppermute(
                    chunk, "seq", [(s, (s + shift) % seq_ways) for s in range(seq_ways)]
                )
            elif shift > 0:
                base = section * seq_ways
                chunk = lax.ppermute(
                    chunk,
                    ("pipe", "seq"),
                    [(base + s, base + (s + shift) % seq_ways) for s in range(seq_ways)],
                )
            source = (seq_index + seq_ways - shift) % seq_ways
            result = lax.dynamic_update_slice_in_dim(
                result, chunk, source * concat_size, axis=concat_axis
            )
        return result

    def to_blocks(head_rows):
        return head_rows.reshape(local_heads, block_count, BLK, DH)

    def head_major(rows):
        return jnp.transpose(rows.reshape(tok_rows, head_count, DH), (1, 0, 2))

    is_last = section_index == last_section
    second = jnp.where(is_last, head_major(cotangent), head_major(inputs[0]))
    stacked = jnp.stack([head_major(queries[0]), second])
    stacked_heads = transpose_seq(stacked, 1, 2)
    query_blocks = to_blocks(stacked_heads[0])
    cot_blocks = to_blocks(stacked_heads[1])
    last_inputs = transpose_seq(head_major(inputs[0]), 0, 1, section=last_section)
    input_heads = jnp.where(is_last, last_inputs, stacked_heads[1])
    values_both = key_pair(to_blocks(input_heads))
    kv_pick = (jnp.arange(seq_ways) * local_heads) // group_size
    key_rows = jnp.transpose(key_heads[0].reshape(tok_rows, kv_count, DH), (1, 0, 2))[kv_pick]
    key_flat = lax.all_to_all(key_rows, "seq", split_axis=0, concat_axis=1, tiled=True)
    key_blocks = jnp.broadcast_to(
        key_flat.reshape(1, block_count, BLK, DH), (local_heads, block_count, BLK, DH)
    )
    keys_both = key_pair(key_blocks)
    allowed = visible(lengths, block_count, BLK)
    softmax_probs = probabilities(query_blocks, keys_both, allowed, score_scale)
    probs_low = softmax_probs.astype(jnp.bfloat16)

    grad_ins = []
    grad_outs = []
    grad_in = cot_blocks
    for tick in range(section_count):
        sender = last_section - tick
        new_grad = value_grad(probs_low, grad_in, BLK, seq_ways)
        grad_ins.append(grad_in)
        grad_outs.append(new_grad)
        if sender > 0:
            grad_in = lax.ppermute(new_grad, "pipe", [(sender, sender - 1)])

    def by_section(per_tick):
        chosen = per_tick[0]
        for tick in range(1, section_count):
            chosen = jnp.where(section_index == last_section - tick, per_tick[tick], chosen)
        return chosen

    held_in = by_section(grad_ins)
    held_out = by_section(grad_outs)
    grad_query, grad_key = weight_grads(
        softmax_probs,
        probs_low,
        query_blocks,
        keys_both,
        values_both,
        held_in,
        score_scale,
        BLK,
    )
    pair = jnp.stack([grad_query, held_out]).reshape(2, local_heads, seq_len, DH)
    pair_out = transpose_seq(pair, 2, 1)
    pair_rows = jnp.transpose(pair_out, (0, 2, 1, 3)).reshape(2, tok_rows, full_width)
    if local_heads == 1:
        key_part = grad_key.reshape(seq_len, DH)
    else:
        key_part = jnp.sum(grad_key.astype(jnp.float32), axis=0).reshape(seq_len, DH)
    key_out = transpose_seq(key_part[:, None, :], 0, 1)
    key_sum = jnp.sum(
        key_out.reshape(tok_rows, kv_count, seq_ways // kv_count, DH).astype(jnp.float32), axis=2
    )
    key_final = key_sum.astype(jnp.bfloat16).reshape(tok_rows, kv_count * DH)
    return (pair_rows[0][None], key_final[None], pair_rows[1][None])


def solution(mesh):
    placed = (
        P("pipe", "seq", None),
        P("pipe", "seq", None),
        P("pipe", "seq", None),
        P("seq", None),
        P(),
    )
    return jax.shard_map(
        on_device,
        mesh=mesh,
        in_specs=placed,
        out_specs=(P("pipe", "seq", None), P("pipe", "seq", None), P("pipe", "seq", None)),
        check_vma=False,
    )
```

```python
import jax
import jax.numpy as jnp
from jax import lax
from jax.sharding import PartitionSpec as P

DH = 128
BLK = 128


def key_pair(block_rows):
    first_block = jnp.broadcast_to(block_rows[:, :1], block_rows.shape)
    return jnp.concatenate([first_block, block_rows], axis=2)


def visible(lengths, block_count, block_len):
    shape = (block_count, block_len, 2 * block_len)
    row_index = lax.broadcasted_iota(jnp.int32, shape, 1)
    col_index = lax.broadcasted_iota(jnp.int32, shape, 2)
    block_index = lax.broadcasted_iota(jnp.int32, shape, 0)
    in_first = col_index < block_len
    offset = jnp.where(in_first, col_index, col_index - block_len)
    own_len = lengths[:, None, None]
    first_ok = in_first & (offset < lengths[0]) & ((block_index > 0) | (offset <= row_index))
    own_ok = (
        jnp.logical_not(in_first) & (block_index > 0) & (offset <= row_index) & (offset < own_len)
    )
    return (first_ok | own_ok)[None]


def fold_keys(key_terms, block_len):
    own_part = key_terms[:, :, block_len:]
    first_part = jnp.sum(key_terms[:, :, :block_len], axis=1)
    return own_part.at[:, 0].add(first_part)


def fold_value(key_terms, block_len, groups):
    own_part = key_terms[:, :, block_len:]
    first_terms = key_terms[:, :, :block_len]
    heads, blocks = first_terms.shape[:2]
    grouped = first_terms.reshape((heads, groups, blocks // groups) + first_terms.shape[2:])
    partial_low = lax.optimization_barrier(jnp.sum(grouped, axis=2).astype(jnp.bfloat16))
    first_part = jnp.sum(partial_low.astype(jnp.float32), axis=1)
    return own_part.at[:, 0].add(first_part)


def probabilities(query_blocks, keys_both, allowed, score_scale):
    scores = (
        jnp.einsum("hbid,hbjd->hbij", query_blocks, keys_both, preferred_element_type=jnp.float32)
        * score_scale
    )
    scores = jnp.where(allowed, scores, -jnp.inf)
    row_max = jnp.max(scores, axis=-1, keepdims=True)
    exp_scores = jnp.exp(scores - row_max)
    return exp_scores / jnp.sum(exp_scores, axis=-1, keepdims=True)


def value_grad(probs_low, grad_blocks, block_len, groups):
    key_terms = jnp.einsum(
        "hbij,hbid->hbjd", probs_low, grad_blocks, preferred_element_type=jnp.float32
    )
    return (grad_blocks.astype(jnp.float32) + fold_value(key_terms, block_len, groups)).astype(
        jnp.bfloat16
    )


def weight_grads(
    softmax_probs, probs_low, query_blocks, keys_both, values_both, grad_blocks, score_scale, block_len
):
    output = jnp.einsum(
        "hbij,hbjd->hbid", probs_low, values_both, preferred_element_type=jnp.float32
    )
    row_dot = jnp.sum(grad_blocks.astype(jnp.float32) * output, axis=-1)[..., None]
    grad_probs = jnp.einsum(
        "hbid,hbjd->hbij", grad_blocks, values_both, preferred_element_type=jnp.float32
    )
    grad_scores = (softmax_probs * (grad_probs - row_dot)).astype(jnp.bfloat16)
    grad_query = (
        jnp.einsum("hbij,hbjd->hbid", grad_scores, keys_both, preferred_element_type=jnp.float32)
        * score_scale
    ).astype(jnp.bfloat16)
    key_terms = jnp.einsum(
        "hbij,hbid->hbjd", grad_scores, query_blocks, preferred_element_type=jnp.float32
    )
    grad_key = (fold_keys(key_terms, block_len) * score_scale).astype(jnp.bfloat16)
    return (grad_query, grad_key)


def on_device(queries, key_heads, inputs, cotangent, lengths):
    section_count = lax.axis_size("pipe")
    section_index = lax.axis_index("pipe")
    seq_ways = lax.axis_size("seq")
    tok_rows = queries.shape[1]
    full_width = queries.shape[2]
    head_count = full_width // DH
    kv_count = key_heads.shape[2] // DH
    group_size = head_count // kv_count
    seq_len = tok_rows * seq_ways
    block_count = seq_len // BLK
    local_heads = head_count // seq_ways
    score_scale = DH ** (-0.5)
    last_section = section_count - 1

    seq_index = lax.axis_index("seq")

    def transpose_seq(value, split_axis, concat_axis, section=None):
        if seq_ways > 8:
            return lax.all_to_all(value, "seq", split_axis, concat_axis, tiled=True)
        split_size = value.shape[split_axis] // seq_ways
        concat_size = value.shape[concat_axis]
        out_shape = list(value.shape)
        out_shape[split_axis] = split_size
        out_shape[concat_axis] = concat_size * seq_ways
        result = jnp.zeros(out_shape, value.dtype)
        if seq_ways == 8:
            shifts = (0, 1, 7, 3, 5, 2, 6, 4)
        else:
            shifts = tuple(range(seq_ways))
        for shift in shifts:
            target = (seq_index + shift) % seq_ways
            chunk = lax.dynamic_slice_in_dim(value, target * split_size, split_size, axis=split_axis)
            if shift > 0 and section is None:
                chunk = lax.ppermute(
                    chunk, "seq", [(s, (s + shift) % seq_ways) for s in range(seq_ways)]
                )
            elif shift > 0:
                base = section * seq_ways
                chunk = lax.ppermute(
                    chunk,
                    ("pipe", "seq"),
                    [(base + s, base + (s + shift) % seq_ways) for s in range(seq_ways)],
                )
            source = (seq_index + seq_ways - shift) % seq_ways
            result = lax.dynamic_update_slice_in_dim(
                result, chunk, source * concat_size, axis=concat_axis
            )
        return result

    def to_blocks(head_rows):
        return head_rows.reshape(local_heads, block_count, BLK, DH)

    def head_major(rows):
        return jnp.transpose(rows.reshape(tok_rows, head_count, DH), (1, 0, 2))

    is_last = section_index == last_section
    second = jnp.where(is_last, head_major(cotangent), head_major(inputs[0]))
    stacked = jnp.stack([head_major(queries[0]), second])
    stacked_heads = transpose_seq(stacked, 1, 2)
    query_blocks = to_blocks(stacked_heads[0])
    cot_blocks = to_blocks(stacked_heads[1])
    last_inputs = transpose_seq(head_major(inputs[0]), 0, 1, section=last_section)
    input_heads = jnp.where(is_last, last_inputs, stacked_heads[1])
    values_both = key_pair(to_blocks(input_heads))
    kv_pick = (jnp.arange(seq_ways) * local_heads) // group_size
    key_rows = jnp.transpose(key_heads[0].reshape(tok_rows, kv_count, DH), (1, 0, 2))[kv_pick]
    key_flat = lax.all_to_all(key_rows, "seq", split_axis=0, concat_axis=1, tiled=True)
    key_blocks = jnp.broadcast_to(
        key_flat.reshape(1, block_count, BLK, DH), (local_heads, block_count, BLK, DH)
    )
    keys_both = key_pair(key_blocks)
    allowed = visible(lengths, block_count, BLK)
    softmax_probs = probabilities(query_blocks, keys_both, allowed, score_scale)
    probs_low = softmax_probs.astype(jnp.bfloat16)

    grad_ins = []
    grad_outs = []
    grad_in = cot_blocks
    for tick in range(section_count):
        sender = last_section - tick
        new_grad = value_grad(probs_low, grad_in, BLK, seq_ways)
        grad_ins.append(grad_in)
        grad_outs.append(new_grad)
        if sender > 0:
            grad_in = lax.ppermute(new_grad, "pipe", [(sender, sender - 1)])

    def by_section(per_tick):
        chosen = per_tick[0]
        for tick in range(1, section_count):
            chosen = jnp.where(section_index == last_section - tick, per_tick[tick], chosen)
        return chosen

    held_in = by_section(grad_ins)
    held_out = by_section(grad_outs)
    grad_query, grad_key = weight_grads(
        softmax_probs,
        probs_low,
        query_blocks,
        keys_both,
        values_both,
        held_in,
        score_scale,
        BLK,
    )
    pair = jnp.stack([grad_query, held_out]).reshape(2, local_heads, seq_len, DH)
    pair_out = transpose_seq(pair, 2, 1)
    pair_rows = jnp.transpose(pair_out, (0, 2, 1, 3)).reshape(2, tok_rows, full_width)
    if local_heads == 1:
        key_part = grad_key.reshape(seq_len, DH)
    else:
        key_part = jnp.sum(grad_key.astype(jnp.float32), axis=0).reshape(seq_len, DH)
    key_out = lax.all_to_all(key_part[:, None, :], "seq", split_axis=0, concat_axis=1, tiled=True)
    key_sum = jnp.sum(
        key_out.reshape(tok_rows, kv_count, seq_ways // kv_count, DH).astype(jnp.float32), axis=2
    )
    key_final = key_sum.astype(jnp.bfloat16).reshape(tok_rows, kv_count * DH)
    return (pair_rows[0][None], key_final[None], pair_rows[1][None])


def solution(mesh):
    placed = (
        P("pipe", "seq", None),
        P("pipe", "seq", None),
        P("pipe", "seq", None),
        P("seq", None),
        P(),
    )
    return jax.shard_map(
        on_device,
        mesh=mesh,
        in_specs=placed,
        out_specs=(P("pipe", "seq", None), P("pipe", "seq", None), P("pipe", "seq", None)),
        check_vma=False,
    )
```

```python
import jax
import jax.numpy as jnp
from jax import lax
from jax.sharding import PartitionSpec as P

DH = 128
BLK = 128


def key_pair(block_rows):
    first_block = jnp.broadcast_to(block_rows[:, :1], block_rows.shape)
    return jnp.concatenate([first_block, block_rows], axis=2)


def visible(lengths, block_count, block_len):
    shape = (block_count, block_len, 2 * block_len)
    row_index = lax.broadcasted_iota(jnp.int32, shape, 1)
    col_index = lax.broadcasted_iota(jnp.int32, shape, 2)
    block_index = lax.broadcasted_iota(jnp.int32, shape, 0)
    in_first = col_index < block_len
    offset = jnp.where(in_first, col_index, col_index - block_len)
    own_len = lengths[:, None, None]
    first_ok = in_first & (offset < lengths[0]) & ((block_index > 0) | (offset <= row_index))
    own_ok = (
        jnp.logical_not(in_first) & (block_index > 0) & (offset <= row_index) & (offset < own_len)
    )
    return (first_ok | own_ok)[None]


def fold_keys(key_terms, block_len):
    own_part = key_terms[:, :, block_len:]
    first_part = jnp.sum(key_terms[:, :, :block_len], axis=1)
    return own_part.at[:, 0].add(first_part)


def fold_value(key_terms, block_len, groups):
    own_part = key_terms[:, :, block_len:]
    first_terms = key_terms[:, :, :block_len]
    heads, blocks = first_terms.shape[:2]
    grouped = first_terms.reshape((heads, groups, blocks // groups) + first_terms.shape[2:])
    partial_low = lax.optimization_barrier(jnp.sum(grouped, axis=2).astype(jnp.bfloat16))
    first_part = jnp.sum(partial_low.astype(jnp.float32), axis=1)
    return own_part.at[:, 0].add(first_part)


def probabilities(query_blocks, keys_both, allowed, score_scale):
    scores = (
        jnp.einsum("hbid,hbjd->hbij", query_blocks, keys_both, preferred_element_type=jnp.float32)
        * score_scale
    )
    scores = jnp.where(allowed, scores, -jnp.inf)
    row_max = jnp.max(scores, axis=-1, keepdims=True)
    exp_scores = jnp.exp(scores - row_max)
    return exp_scores / jnp.sum(exp_scores, axis=-1, keepdims=True)


def value_grad(probs_low, grad_blocks, block_len, groups):
    key_terms = jnp.einsum(
        "hbij,hbid->hbjd", probs_low, grad_blocks, preferred_element_type=jnp.float32
    )
    return (grad_blocks.astype(jnp.float32) + fold_value(key_terms, block_len, groups)).astype(
        jnp.bfloat16
    )


def weight_grads(
    softmax_probs, probs_low, query_blocks, keys_both, values_both, grad_blocks, score_scale, block_len
):
    output = jnp.einsum(
        "hbij,hbjd->hbid", probs_low, values_both, preferred_element_type=jnp.float32
    )
    row_dot = jnp.sum(grad_blocks.astype(jnp.float32) * output, axis=-1)[..., None]
    grad_probs = jnp.einsum(
        "hbid,hbjd->hbij", grad_blocks, values_both, preferred_element_type=jnp.float32
    )
    grad_scores = (softmax_probs * (grad_probs - row_dot)).astype(jnp.bfloat16)
    grad_query = (
        jnp.einsum("hbij,hbjd->hbid", grad_scores, keys_both, preferred_element_type=jnp.float32)
        * score_scale
    ).astype(jnp.bfloat16)
    key_terms = jnp.einsum(
        "hbij,hbid->hbjd", grad_scores, query_blocks, preferred_element_type=jnp.float32
    )
    grad_key = (fold_keys(key_terms, block_len) * score_scale).astype(jnp.bfloat16)
    return (grad_query, grad_key)


def on_device(queries, key_heads, inputs, cotangent, lengths):
    section_count = lax.axis_size("pipe")
    section_index = lax.axis_index("pipe")
    seq_ways = lax.axis_size("seq")
    tok_rows = queries.shape[1]
    full_width = queries.shape[2]
    head_count = full_width // DH
    kv_count = key_heads.shape[2] // DH
    group_size = head_count // kv_count
    seq_len = tok_rows * seq_ways
    block_count = seq_len // BLK
    local_heads = head_count // seq_ways
    score_scale = DH ** (-0.5)
    last_section = section_count - 1

    seq_index = lax.axis_index("seq")

    def transpose_seq(value, split_axis, concat_axis, section=None):
        if seq_ways > 8:
            return lax.all_to_all(value, "seq", split_axis, concat_axis, tiled=True)
        split_size = value.shape[split_axis] // seq_ways
        concat_size = value.shape[concat_axis]
        out_shape = list(value.shape)
        out_shape[split_axis] = split_size
        out_shape[concat_axis] = concat_size * seq_ways
        result = jnp.zeros(out_shape, value.dtype)
        for shift in range(seq_ways):
            target = (seq_index + shift) % seq_ways
            chunk = lax.dynamic_slice_in_dim(value, target * split_size, split_size, axis=split_axis)
            if shift > 0 and section is None:
                chunk = lax.ppermute(
                    chunk, "seq", [(s, (s + shift) % seq_ways) for s in range(seq_ways)]
                )
            elif shift > 0:
                base = section * seq_ways
                chunk = lax.ppermute(
                    chunk,
                    ("pipe", "seq"),
                    [(base + s, base + (s + shift) % seq_ways) for s in range(seq_ways)],
                )
            source = (seq_index + seq_ways - shift) % seq_ways
            result = lax.dynamic_update_slice_in_dim(
                result, chunk, source * concat_size, axis=concat_axis
            )
        return result

    def to_blocks(head_rows):
        return head_rows.reshape(local_heads, block_count, BLK, DH)

    def head_major(rows):
        return jnp.transpose(rows.reshape(tok_rows, head_count, DH), (1, 0, 2))

    is_last = section_index == last_section
    second = jnp.where(is_last, head_major(cotangent), head_major(inputs[0]))
    stacked = jnp.stack([head_major(queries[0]), second])
    stacked_heads = transpose_seq(stacked, 1, 2)
    query_blocks = to_blocks(stacked_heads[0])
    cot_blocks = to_blocks(stacked_heads[1])
    last_inputs = transpose_seq(head_major(inputs[0]), 0, 1, section=last_section)
    input_heads = jnp.where(is_last, last_inputs, stacked_heads[1])
    values_both = key_pair(to_blocks(input_heads))
    kv_pick = (jnp.arange(seq_ways) * local_heads) // group_size
    key_rows = jnp.transpose(key_heads[0].reshape(tok_rows, kv_count, DH), (1, 0, 2))[kv_pick]
    key_flat = lax.all_to_all(key_rows, "seq", split_axis=0, concat_axis=1, tiled=True)
    key_blocks = jnp.broadcast_to(
        key_flat.reshape(1, block_count, BLK, DH), (local_heads, block_count, BLK, DH)
    )
    keys_both = key_pair(key_blocks)
    allowed = visible(lengths, block_count, BLK)
    softmax_probs = probabilities(query_blocks, keys_both, allowed, score_scale)
    probs_low = softmax_probs.astype(jnp.bfloat16)

    grad_ins = []
    grad_outs = []
    grad_in = cot_blocks
    for tick in range(section_count):
        sender = last_section - tick
        new_grad = value_grad(probs_low, grad_in, BLK, seq_ways)
        grad_ins.append(grad_in)
        grad_outs.append(new_grad)
        if sender > 0:
            grad_in = lax.ppermute(new_grad, "pipe", [(sender, sender - 1)])

    def by_section(per_tick):
        chosen = per_tick[0]
        for tick in range(1, section_count):
            chosen = jnp.where(section_index == last_section - tick, per_tick[tick], chosen)
        return chosen

    held_in = by_section(grad_ins)
    held_out = by_section(grad_outs)
    grad_query, grad_key = weight_grads(
        softmax_probs,
        probs_low,
        query_blocks,
        keys_both,
        values_both,
        held_in,
        score_scale,
        BLK,
    )
    pair = jnp.stack([grad_query, held_out]).reshape(2, local_heads, seq_len, DH)
    pair_out = transpose_seq(pair, 2, 1)
    pair_rows = jnp.transpose(pair_out, (0, 2, 1, 3)).reshape(2, tok_rows, full_width)
    if local_heads == 1:
        key_part = grad_key.reshape(seq_len, DH)
    else:
        key_part = jnp.sum(grad_key.astype(jnp.float32), axis=0).reshape(seq_len, DH)
    if seq_ways == 8 and seq_ways // kv_count == 2:
        parity = seq_index % 2
        by_parity = key_part.reshape(seq_ways // 2, 2, tok_rows, DH)
        keep = lax.dynamic_index_in_dim(by_parity, parity, axis=1, keepdims=False)
        give = lax.dynamic_index_in_dim(by_parity, 1 - parity, axis=1, keepdims=False)
        got = lax.ppermute(give, "seq", [(d, d ^ 1) for d in range(seq_ways)])
        kept_sum = keep + got
        received = []
        for shift in range(0, seq_ways, 2):
            block = ((seq_index + shift) % seq_ways) // 2
            chunk = lax.dynamic_index_in_dim(kept_sum, block, axis=0, keepdims=False)
            if shift > 0:
                chunk = lax.ppermute(
                    chunk, "seq", [(d, (d + shift) % seq_ways) for d in range(seq_ways)]
                )
            received.append(chunk)
        heads_in = jnp.arange(kv_count)
        order = ((seq_index - 2 * heads_in - parity) % seq_ways) // 2
        key_sum = jnp.transpose(jnp.take(jnp.stack(received), order, axis=0), (1, 0, 2))
    else:
        key_out = lax.all_to_all(
            key_part[:, None, :], "seq", split_axis=0, concat_axis=1, tiled=True
        )
        key_sum = jnp.sum(
            key_out.reshape(tok_rows, kv_count, seq_ways // kv_count, DH).astype(jnp.float32),
            axis=2,
        )
    key_final = key_sum.astype(jnp.bfloat16).reshape(tok_rows, kv_count * DH)
    return (pair_rows[0][None], key_final[None], pair_rows[1][None])


def solution(mesh):
    placed = (
        P("pipe", "seq", None),
        P("pipe", "seq", None),
        P("pipe", "seq", None),
        P("seq", None),
        P(),
    )
    return jax.shard_map(
        on_device,
        mesh=mesh,
        in_specs=placed,
        out_specs=(P("pipe", "seq", None), P("pipe", "seq", None), P("pipe", "seq", None)),
        check_vma=False,
    )
```

```python
import jax
import jax.numpy as jnp
from jax import lax
from jax.sharding import PartitionSpec as P

DH = 128
BLK = 128


def key_pair(block_rows):
    first_block = jnp.broadcast_to(block_rows[:, :1], block_rows.shape)
    return jnp.concatenate([first_block, block_rows], axis=2)


def visible(lengths, block_count, block_len):
    shape = (block_count, block_len, 2 * block_len)
    row_index = lax.broadcasted_iota(jnp.int32, shape, 1)
    col_index = lax.broadcasted_iota(jnp.int32, shape, 2)
    block_index = lax.broadcasted_iota(jnp.int32, shape, 0)
    in_first = col_index < block_len
    offset = jnp.where(in_first, col_index, col_index - block_len)
    own_len = lengths[:, None, None]
    first_ok = in_first & (offset < lengths[0]) & ((block_index > 0) | (offset <= row_index))
    own_ok = (
        jnp.logical_not(in_first) & (block_index > 0) & (offset <= row_index) & (offset < own_len)
    )
    return (first_ok | own_ok)[None]


def fold_keys(key_terms, block_len):
    own_part = key_terms[:, :, block_len:]
    first_part = jnp.sum(key_terms[:, :, :block_len], axis=1)
    return own_part.at[:, 0].add(first_part)


def fold_value(key_terms, block_len, groups):
    own_part = key_terms[:, :, block_len:]
    first_terms = key_terms[:, :, :block_len]
    heads, blocks = first_terms.shape[:2]
    grouped = first_terms.reshape((heads, groups, blocks // groups) + first_terms.shape[2:])
    partial_low = lax.optimization_barrier(jnp.sum(grouped, axis=2).astype(jnp.bfloat16))
    first_part = jnp.sum(partial_low.astype(jnp.float32), axis=1)
    return own_part.at[:, 0].add(first_part)


def probabilities(query_blocks, keys_both, allowed, score_scale):
    scores = (
        jnp.einsum("hbid,hbjd->hbij", query_blocks, keys_both, preferred_element_type=jnp.float32)
        * score_scale
    )
    scores = jnp.where(allowed, scores, -jnp.inf)
    row_max = jnp.max(scores, axis=-1, keepdims=True)
    exp_scores = jnp.exp(scores - row_max)
    return exp_scores / jnp.sum(exp_scores, axis=-1, keepdims=True)


def value_grad(probs_low, grad_blocks, block_len, groups):
    key_terms = jnp.einsum(
        "hbij,hbid->hbjd", probs_low, grad_blocks, preferred_element_type=jnp.float32
    )
    return (grad_blocks.astype(jnp.float32) + fold_value(key_terms, block_len, groups)).astype(
        jnp.bfloat16
    )


def weight_grads(
    softmax_probs, probs_low, query_blocks, keys_both, values_both, grad_blocks, score_scale, block_len
):
    output = jnp.einsum(
        "hbij,hbjd->hbid", probs_low, values_both, preferred_element_type=jnp.float32
    )
    row_dot = jnp.sum(grad_blocks.astype(jnp.float32) * output, axis=-1)[..., None]
    grad_probs = jnp.einsum(
        "hbid,hbjd->hbij", grad_blocks, values_both, preferred_element_type=jnp.float32
    )
    grad_scores = (softmax_probs * (grad_probs - row_dot)).astype(jnp.bfloat16)
    grad_query = (
        jnp.einsum("hbij,hbjd->hbid", grad_scores, keys_both, preferred_element_type=jnp.float32)
        * score_scale
    ).astype(jnp.bfloat16)
    key_terms = jnp.einsum(
        "hbij,hbid->hbjd", grad_scores, query_blocks, preferred_element_type=jnp.float32
    )
    grad_key = (fold_keys(key_terms, block_len) * score_scale).astype(jnp.bfloat16)
    return (grad_query, grad_key)


def on_device(queries, key_heads, inputs, cotangent, lengths):
    section_count = lax.axis_size("pipe")
    section_index = lax.axis_index("pipe")
    seq_ways = lax.axis_size("seq")
    tok_rows = queries.shape[1]
    full_width = queries.shape[2]
    head_count = full_width // DH
    kv_count = key_heads.shape[2] // DH
    group_size = head_count // kv_count
    seq_len = tok_rows * seq_ways
    block_count = seq_len // BLK
    local_heads = head_count // seq_ways
    score_scale = DH ** (-0.5)
    last_section = section_count - 1

    seq_index = lax.axis_index("seq")

    def transpose_seq(value, split_axis, concat_axis, section=None):
        if seq_ways > 8:
            return lax.all_to_all(value, "seq", split_axis, concat_axis, tiled=True)
        split_size = value.shape[split_axis] // seq_ways
        concat_size = value.shape[concat_axis]
        out_shape = list(value.shape)
        out_shape[split_axis] = split_size
        out_shape[concat_axis] = concat_size * seq_ways
        result = jnp.zeros(out_shape, value.dtype)
        for shift in range(seq_ways):
            target = (seq_index + shift) % seq_ways
            chunk = lax.dynamic_slice_in_dim(value, target * split_size, split_size, axis=split_axis)
            if shift > 0 and section is None:
                chunk = lax.ppermute(
                    chunk, "seq", [(s, (s + shift) % seq_ways) for s in range(seq_ways)]
                )
            elif shift > 0:
                base = section * seq_ways
                chunk = lax.ppermute(
                    chunk,
                    ("pipe", "seq"),
                    [(base + s, base + (s + shift) % seq_ways) for s in range(seq_ways)],
                )
            source = (seq_index + seq_ways - shift) % seq_ways
            result = lax.dynamic_update_slice_in_dim(
                result, chunk, source * concat_size, axis=concat_axis
            )
        return result

    def to_blocks(head_rows):
        return head_rows.reshape(local_heads, block_count, BLK, DH)

    def head_major(rows):
        return jnp.transpose(rows.reshape(tok_rows, head_count, DH), (1, 0, 2))

    is_last = section_index == last_section
    second = jnp.where(is_last, head_major(cotangent), head_major(inputs[0]))
    stacked = jnp.stack([head_major(queries[0]), second])
    stacked_heads = transpose_seq(stacked, 1, 2)
    query_blocks = to_blocks(stacked_heads[0])
    cot_blocks = to_blocks(stacked_heads[1])
    last_inputs = transpose_seq(head_major(inputs[0]), 0, 1, section=last_section)
    input_heads = jnp.where(is_last, last_inputs, stacked_heads[1])
    values_both = key_pair(to_blocks(input_heads))
    kv_rows = jnp.transpose(key_heads[0].reshape(tok_rows, kv_count, DH), (1, 0, 2))
    if seq_ways == 8 and seq_ways // kv_count == 2:
        parity = seq_index % 2
        fetched = []
        for shift in range(0, seq_ways, 2):
            head = ((seq_index + shift) % seq_ways) // 2
            chunk = lax.dynamic_index_in_dim(kv_rows, head, axis=0, keepdims=False)
            if shift > 0:
                chunk = lax.ppermute(
                    chunk, "seq", [(d, (d + shift) % seq_ways) for d in range(seq_ways)]
                )
            fetched.append(chunk)
        mine = jnp.stack(fetched)
        theirs = lax.ppermute(mine, "seq", [(d, d ^ 1) for d in range(seq_ways)])
        partner = seq_index + 1 - 2 * parity
        blocks = jnp.arange(seq_ways)
        order = jnp.where(
            blocks % 2 == parity,
            ((seq_index - blocks) % seq_ways) // 2,
            seq_ways // 2 + ((partner - blocks) % seq_ways) // 2,
        )
        key_flat = jnp.take(jnp.concatenate([mine, theirs]), order, axis=0).reshape(1, seq_len, DH)
    else:
        kv_pick = (jnp.arange(seq_ways) * local_heads) // group_size
        key_flat = lax.all_to_all(kv_rows[kv_pick], "seq", split_axis=0, concat_axis=1, tiled=True)
    key_blocks = jnp.broadcast_to(
        key_flat.reshape(1, block_count, BLK, DH), (local_heads, block_count, BLK, DH)
    )
    keys_both = key_pair(key_blocks)
    allowed = visible(lengths, block_count, BLK)
    softmax_probs = probabilities(query_blocks, keys_both, allowed, score_scale)
    probs_low = softmax_probs.astype(jnp.bfloat16)

    grad_ins = []
    grad_outs = []
    grad_in = cot_blocks
    for tick in range(section_count):
        sender = last_section - tick
        new_grad = value_grad(probs_low, grad_in, BLK, seq_ways)
        grad_ins.append(grad_in)
        grad_outs.append(new_grad)
        if sender > 0:
            grad_in = lax.ppermute(new_grad, "pipe", [(sender, sender - 1)])

    def by_section(per_tick):
        chosen = per_tick[0]
        for tick in range(1, section_count):
            chosen = jnp.where(section_index == last_section - tick, per_tick[tick], chosen)
        return chosen

    held_in = by_section(grad_ins)
    held_out = by_section(grad_outs)
    grad_query, grad_key = weight_grads(
        softmax_probs,
        probs_low,
        query_blocks,
        keys_both,
        values_both,
        held_in,
        score_scale,
        BLK,
    )
    pair = jnp.stack([grad_query, held_out]).reshape(2, local_heads, seq_len, DH)
    pair_out = transpose_seq(pair, 2, 1)
    pair_rows = jnp.transpose(pair_out, (0, 2, 1, 3)).reshape(2, tok_rows, full_width)
    if local_heads == 1:
        key_part = grad_key.reshape(seq_len, DH)
    else:
        key_part = jnp.sum(grad_key.astype(jnp.float32), axis=0).reshape(seq_len, DH)
    if seq_ways == 8 and seq_ways // kv_count == 2:
        parity = seq_index % 2
        by_parity = key_part.reshape(seq_ways // 2, 2, tok_rows, DH)
        keep = lax.dynamic_index_in_dim(by_parity, parity, axis=1, keepdims=False)
        give = lax.dynamic_index_in_dim(by_parity, 1 - parity, axis=1, keepdims=False)
        got = lax.ppermute(give, "seq", [(d, d ^ 1) for d in range(seq_ways)])
        kept_sum = keep + got
        received = []
        for shift in range(0, seq_ways, 2):
            block = ((seq_index + shift) % seq_ways) // 2
            chunk = lax.dynamic_index_in_dim(kept_sum, block, axis=0, keepdims=False)
            if shift > 0:
                chunk = lax.ppermute(
                    chunk, "seq", [(d, (d + shift) % seq_ways) for d in range(seq_ways)]
                )
            received.append(chunk)
        heads_in = jnp.arange(kv_count)
        order = ((seq_index - 2 * heads_in - parity) % seq_ways) // 2
        key_sum = jnp.transpose(jnp.take(jnp.stack(received), order, axis=0), (1, 0, 2))
    else:
        key_out = lax.all_to_all(
            key_part[:, None, :], "seq", split_axis=0, concat_axis=1, tiled=True
        )
        key_sum = jnp.sum(
            key_out.reshape(tok_rows, kv_count, seq_ways // kv_count, DH).astype(jnp.float32),
            axis=2,
        )
    key_final = key_sum.astype(jnp.bfloat16).reshape(tok_rows, kv_count * DH)
    return (pair_rows[0][None], key_final[None], pair_rows[1][None])


def solution(mesh):
    placed = (
        P("pipe", "seq", None),
        P("pipe", "seq", None),
        P("pipe", "seq", None),
        P("seq", None),
        P(),
    )
    return jax.shard_map(
        on_device,
        mesh=mesh,
        in_specs=placed,
        out_specs=(P("pipe", "seq", None), P("pipe", "seq", None), P("pipe", "seq", None)),
        check_vma=False,
    )
```

```python
import jax
import jax.numpy as jnp
from jax import lax
from jax.sharding import PartitionSpec as P

DH = 128
BLK = 128


def key_pair(block_rows):
    first_block = jnp.broadcast_to(block_rows[:, :1], block_rows.shape)
    return jnp.concatenate([first_block, block_rows], axis=2)


def visible(lengths, block_count, block_len):
    shape = (block_count, block_len, 2 * block_len)
    row_index = lax.broadcasted_iota(jnp.int32, shape, 1)
    col_index = lax.broadcasted_iota(jnp.int32, shape, 2)
    block_index = lax.broadcasted_iota(jnp.int32, shape, 0)
    in_first = col_index < block_len
    offset = jnp.where(in_first, col_index, col_index - block_len)
    own_len = lengths[:, None, None]
    first_ok = in_first & (offset < lengths[0]) & ((block_index > 0) | (offset <= row_index))
    own_ok = (
        jnp.logical_not(in_first) & (block_index > 0) & (offset <= row_index) & (offset < own_len)
    )
    return (first_ok | own_ok)[None]


def fold_keys(key_terms, block_len):
    own_part = key_terms[:, :, block_len:]
    first_part = jnp.sum(key_terms[:, :, :block_len], axis=1)
    return own_part.at[:, 0].add(first_part)


def fold_value(key_terms, block_len, groups):
    own_part = key_terms[:, :, block_len:]
    first_terms = key_terms[:, :, :block_len]
    heads, blocks = first_terms.shape[:2]
    grouped = first_terms.reshape((heads, groups, blocks // groups) + first_terms.shape[2:])
    partial_low = lax.optimization_barrier(jnp.sum(grouped, axis=2).astype(jnp.bfloat16))
    first_part = jnp.sum(partial_low.astype(jnp.float32), axis=1)
    return own_part.at[:, 0].add(first_part)


def probabilities(query_blocks, keys_both, allowed, score_scale):
    scores = (
        jnp.einsum("hbid,hbjd->hbij", query_blocks, keys_both, preferred_element_type=jnp.float32)
        * score_scale
    )
    scores = jnp.where(allowed, scores, -jnp.inf)
    row_max = jnp.max(scores, axis=-1, keepdims=True)
    exp_scores = jnp.exp(scores - row_max)
    return exp_scores / jnp.sum(exp_scores, axis=-1, keepdims=True)


def value_grad(probs_low, grad_blocks, block_len, groups):
    key_terms = jnp.einsum(
        "hbij,hbid->hbjd", probs_low, grad_blocks, preferred_element_type=jnp.float32
    )
    return (grad_blocks.astype(jnp.float32) + fold_value(key_terms, block_len, groups)).astype(
        jnp.bfloat16
    )


def weight_grads(
    softmax_probs, probs_low, query_blocks, keys_both, values_both, grad_blocks, score_scale, block_len
):
    output = jnp.einsum(
        "hbij,hbjd->hbid", probs_low, values_both, preferred_element_type=jnp.float32
    )
    row_dot = jnp.sum(grad_blocks.astype(jnp.float32) * output, axis=-1)[..., None]
    grad_probs = jnp.einsum(
        "hbid,hbjd->hbij", grad_blocks, values_both, preferred_element_type=jnp.float32
    )
    grad_scores = (softmax_probs * (grad_probs - row_dot)).astype(jnp.bfloat16)
    grad_query = (
        jnp.einsum("hbij,hbjd->hbid", grad_scores, keys_both, preferred_element_type=jnp.float32)
        * score_scale
    ).astype(jnp.bfloat16)
    key_terms = jnp.einsum(
        "hbij,hbid->hbjd", grad_scores, query_blocks, preferred_element_type=jnp.float32
    )
    grad_key = (fold_keys(key_terms, block_len) * score_scale).astype(jnp.bfloat16)
    return (grad_query, grad_key)


def on_device(queries, key_heads, inputs, cotangent, lengths):
    section_count = lax.axis_size("pipe")
    section_index = lax.axis_index("pipe")
    seq_ways = lax.axis_size("seq")
    tok_rows = queries.shape[1]
    full_width = queries.shape[2]
    head_count = full_width // DH
    kv_count = key_heads.shape[2] // DH
    group_size = head_count // kv_count
    seq_len = tok_rows * seq_ways
    block_count = seq_len // BLK
    local_heads = head_count // seq_ways
    score_scale = DH ** (-0.5)
    last_section = section_count - 1

    seq_index = lax.axis_index("seq")

    def transpose_seq(value, split_axis, concat_axis, section=None):
        if seq_ways > 8:
            return lax.all_to_all(value, "seq", split_axis, concat_axis, tiled=True)
        split_size = value.shape[split_axis] // seq_ways
        concat_size = value.shape[concat_axis]
        out_shape = list(value.shape)
        out_shape[split_axis] = split_size
        out_shape[concat_axis] = concat_size * seq_ways
        result = jnp.zeros(out_shape, value.dtype)
        for shift in range(seq_ways):
            target = (seq_index + shift) % seq_ways
            chunk = lax.dynamic_slice_in_dim(value, target * split_size, split_size, axis=split_axis)
            if shift > 0 and section is None:
                chunk = lax.ppermute(
                    chunk, "seq", [(s, (s + shift) % seq_ways) for s in range(seq_ways)]
                )
            elif shift > 0:
                base = section * seq_ways
                chunk = lax.ppermute(
                    chunk,
                    ("pipe", "seq"),
                    [(base + s, base + (s + shift) % seq_ways) for s in range(seq_ways)],
                )
            source = (seq_index + seq_ways - shift) % seq_ways
            result = lax.dynamic_update_slice_in_dim(
                result, chunk, source * concat_size, axis=concat_axis
            )
        return result

    def to_blocks(head_rows):
        return head_rows.reshape(local_heads, block_count, BLK, DH)

    def head_major(rows):
        return jnp.transpose(rows.reshape(tok_rows, head_count, DH), (1, 0, 2))

    is_last = section_index == last_section
    second = jnp.where(is_last, head_major(cotangent), head_major(inputs[0]))
    stacked = jnp.stack([head_major(queries[0]), second])
    stacked_heads = transpose_seq(stacked, 1, 2)
    query_blocks = to_blocks(stacked_heads[0])
    cot_blocks = to_blocks(stacked_heads[1])
    last_inputs = transpose_seq(head_major(inputs[0]), 0, 1, section=last_section)
    input_heads = jnp.where(is_last, last_inputs, stacked_heads[1])
    values_both = key_pair(to_blocks(input_heads))
    kv_rows = jnp.transpose(key_heads[0].reshape(tok_rows, kv_count, DH), (1, 0, 2))
    if seq_ways == 8 and seq_ways // kv_count == 2:
        parity = seq_index % 2
        fetched = []
        for shift in range(0, seq_ways, 2):
            head = ((seq_index + shift) % seq_ways) // 2
            chunk = lax.dynamic_index_in_dim(kv_rows, head, axis=0, keepdims=False)
            if shift > 0:
                chunk = lax.ppermute(
                    chunk, "seq", [(d, (d + shift) % seq_ways) for d in range(seq_ways)]
                )
            fetched.append(chunk)
        mine = jnp.stack(fetched)
        theirs = lax.ppermute(mine, "seq", [(d, d ^ 1) for d in range(seq_ways)])
        partner = seq_index + 1 - 2 * parity
        blocks = jnp.arange(seq_ways)
        order = jnp.where(
            blocks % 2 == parity,
            ((seq_index - blocks) % seq_ways) // 2,
            seq_ways // 2 + ((partner - blocks) % seq_ways) // 2,
        )
        key_flat = jnp.take(jnp.concatenate([mine, theirs]), order, axis=0).reshape(1, seq_len, DH)
    else:
        kv_pick = (jnp.arange(seq_ways) * local_heads) // group_size
        key_flat = lax.all_to_all(kv_rows[kv_pick], "seq", split_axis=0, concat_axis=1, tiled=True)
    key_blocks = jnp.broadcast_to(
        key_flat.reshape(1, block_count, BLK, DH), (local_heads, block_count, BLK, DH)
    )
    keys_both = key_pair(key_blocks)
    allowed = visible(lengths, block_count, BLK)
    softmax_probs = probabilities(query_blocks, keys_both, allowed, score_scale)
    probs_low = softmax_probs.astype(jnp.bfloat16)

    grad_ins = []
    grad_outs = []
    grad_in = cot_blocks
    for tick in range(section_count):
        sender = last_section - tick
        new_grad = value_grad(probs_low, grad_in, BLK, seq_ways)
        grad_ins.append(grad_in)
        grad_outs.append(new_grad)
        if sender > 0:
            grad_in = lax.ppermute(new_grad, "pipe", [(sender, sender - 1)])

    def by_section(per_tick):
        chosen = per_tick[0]
        for tick in range(1, section_count):
            chosen = jnp.where(section_index == last_section - tick, per_tick[tick], chosen)
        return chosen

    held_in = by_section(grad_ins)
    held_out = by_section(grad_outs)
    grad_query, grad_key = weight_grads(
        softmax_probs,
        probs_low,
        query_blocks,
        keys_both,
        values_both,
        held_in,
        score_scale,
        BLK,
    )
    pair = jnp.transpose(
        jnp.stack([grad_query, held_out]).reshape(2, local_heads, seq_len, DH), (0, 2, 1, 3)
    )
    pair_out = transpose_seq(pair, 1, 2)
    pair_rows = pair_out.reshape(2, tok_rows, full_width)
    if local_heads == 1:
        key_part = grad_key.reshape(seq_len, DH)
    else:
        key_part = jnp.sum(grad_key.astype(jnp.float32), axis=0).reshape(seq_len, DH)
    if seq_ways == 8 and seq_ways // kv_count == 2:
        parity = seq_index % 2
        by_parity = key_part.reshape(seq_ways // 2, 2, tok_rows, DH)
        keep = lax.dynamic_index_in_dim(by_parity, parity, axis=1, keepdims=False)
        give = lax.dynamic_index_in_dim(by_parity, 1 - parity, axis=1, keepdims=False)
        got = lax.ppermute(give, "seq", [(d, d ^ 1) for d in range(seq_ways)])
        kept_sum = keep + got
        received = []
        for shift in range(0, seq_ways, 2):
            block = ((seq_index + shift) % seq_ways) // 2
            chunk = lax.dynamic_index_in_dim(kept_sum, block, axis=0, keepdims=False)
            if shift > 0:
                chunk = lax.ppermute(
                    chunk, "seq", [(d, (d + shift) % seq_ways) for d in range(seq_ways)]
                )
            received.append(chunk)
        heads_in = jnp.arange(kv_count)
        order = ((seq_index - 2 * heads_in - parity) % seq_ways) // 2
        key_sum = jnp.transpose(jnp.take(jnp.stack(received), order, axis=0), (1, 0, 2))
    else:
        key_out = lax.all_to_all(
            key_part[:, None, :], "seq", split_axis=0, concat_axis=1, tiled=True
        )
        key_sum = jnp.sum(
            key_out.reshape(tok_rows, kv_count, seq_ways // kv_count, DH).astype(jnp.float32),
            axis=2,
        )
    key_final = key_sum.astype(jnp.bfloat16).reshape(tok_rows, kv_count * DH)
    return (pair_rows[0][None], key_final[None], pair_rows[1][None])


def solution(mesh):
    placed = (
        P("pipe", "seq", None),
        P("pipe", "seq", None),
        P("pipe", "seq", None),
        P("seq", None),
        P(),
    )
    return jax.shard_map(
        on_device,
        mesh=mesh,
        in_specs=placed,
        out_specs=(P("pipe", "seq", None), P("pipe", "seq", None), P("pipe", "seq", None)),
        check_vma=False,
    )
```

```python
import jax
import jax.numpy as jnp
from jax import lax
from jax.sharding import PartitionSpec as P

DH = 128
BLK = 128


def key_pair(block_rows):
    first_block = jnp.broadcast_to(block_rows[:, :1], block_rows.shape)
    return jnp.concatenate([first_block, block_rows], axis=2)


def visible(lengths, block_count, block_len):
    shape = (block_count, block_len, 2 * block_len)
    row_index = lax.broadcasted_iota(jnp.int32, shape, 1)
    col_index = lax.broadcasted_iota(jnp.int32, shape, 2)
    block_index = lax.broadcasted_iota(jnp.int32, shape, 0)
    in_first = col_index < block_len
    offset = jnp.where(in_first, col_index, col_index - block_len)
    own_len = lengths[:, None, None]
    first_ok = in_first & (offset < lengths[0]) & ((block_index > 0) | (offset <= row_index))
    own_ok = (
        jnp.logical_not(in_first) & (block_index > 0) & (offset <= row_index) & (offset < own_len)
    )
    return (first_ok | own_ok)[None]


def fold_keys(key_terms, block_len):
    own_part = key_terms[:, :, block_len:]
    first_part = jnp.sum(key_terms[:, :, :block_len], axis=1)
    return own_part.at[:, 0].add(first_part)


def fold_value(key_terms, block_len, groups):
    own_part = key_terms[:, :, block_len:]
    first_terms = key_terms[:, :, :block_len]
    heads, blocks = first_terms.shape[:2]
    grouped = first_terms.reshape((heads, groups, blocks // groups) + first_terms.shape[2:])
    partial_low = lax.optimization_barrier(jnp.sum(grouped, axis=2).astype(jnp.bfloat16))
    first_part = jnp.sum(partial_low.astype(jnp.float32), axis=1)
    return own_part.at[:, 0].add(first_part)


def probabilities(query_blocks, keys_both, allowed, score_scale):
    scores = (
        jnp.einsum("hbid,hbjd->hbij", query_blocks, keys_both, preferred_element_type=jnp.float32)
        * score_scale
    )
    scores = jnp.where(allowed, scores, -jnp.inf)
    row_max = jnp.max(scores, axis=-1, keepdims=True)
    exp_scores = jnp.exp(scores - row_max)
    return exp_scores / jnp.sum(exp_scores, axis=-1, keepdims=True)


def value_grad(probs_low, grad_blocks, block_len, groups):
    key_terms = jnp.einsum(
        "hbij,hbid->hbjd", probs_low, grad_blocks, preferred_element_type=jnp.float32
    )
    return (grad_blocks.astype(jnp.float32) + fold_value(key_terms, block_len, groups)).astype(
        jnp.bfloat16
    )


def weight_grads(
    softmax_probs, probs_low, query_blocks, keys_both, values_both, grad_blocks, score_scale, block_len
):
    output = jnp.einsum(
        "hbij,hbjd->hbid", probs_low, values_both, preferred_element_type=jnp.float32
    )
    row_dot = jnp.sum(grad_blocks.astype(jnp.float32) * output, axis=-1)[..., None]
    grad_probs = jnp.einsum(
        "hbid,hbjd->hbij", grad_blocks, values_both, preferred_element_type=jnp.float32
    )
    grad_scores = (softmax_probs * (grad_probs - row_dot)).astype(jnp.bfloat16)
    grad_query = (
        jnp.einsum("hbij,hbjd->hbid", grad_scores, keys_both, preferred_element_type=jnp.float32)
        * score_scale
    ).astype(jnp.bfloat16)
    key_terms = jnp.einsum(
        "hbij,hbid->hbjd", grad_scores, query_blocks, preferred_element_type=jnp.float32
    )
    grad_key = (fold_keys(key_terms, block_len) * score_scale).astype(jnp.bfloat16)
    return (grad_query, grad_key)


def on_device(queries, key_heads, inputs, cotangent, lengths):
    section_count = lax.axis_size("pipe")
    section_index = lax.axis_index("pipe")
    seq_ways = lax.axis_size("seq")
    tok_rows = queries.shape[1]
    full_width = queries.shape[2]
    head_count = full_width // DH
    kv_count = key_heads.shape[2] // DH
    group_size = head_count // kv_count
    seq_len = tok_rows * seq_ways
    block_count = seq_len // BLK
    local_heads = head_count // seq_ways
    score_scale = DH ** (-0.5)
    last_section = section_count - 1

    seq_index = lax.axis_index("seq")

    def transpose_seq(value, split_axis, concat_axis, section=None, apart=False):
        if seq_ways > 8:
            moved = lax.all_to_all(value, "seq", split_axis, concat_axis, tiled=True)
            return [moved[i] for i in range(value.shape[0])] if apart else moved
        split_size = value.shape[split_axis] // seq_ways
        concat_size = value.shape[concat_axis]
        out_shape = list(value.shape)
        out_shape[split_axis] = split_size
        out_shape[concat_axis] = concat_size * seq_ways
        parts = value.shape[0] if apart else 1
        part_shape = out_shape[1:] if apart else out_shape
        results = [jnp.zeros(part_shape, value.dtype) for _ in range(parts)]
        part_axis = concat_axis - 1 if apart else concat_axis
        for shift in range(seq_ways):
            target = (seq_index + shift) % seq_ways
            chunk = lax.dynamic_slice_in_dim(value, target * split_size, split_size, axis=split_axis)
            if shift > 0 and section is None:
                chunk = lax.ppermute(
                    chunk, "seq", [(s, (s + shift) % seq_ways) for s in range(seq_ways)]
                )
            elif shift > 0:
                base = section * seq_ways
                chunk = lax.ppermute(
                    chunk,
                    ("pipe", "seq"),
                    [(base + s, base + (s + shift) % seq_ways) for s in range(seq_ways)],
                )
            source = (seq_index + seq_ways - shift) % seq_ways
            for i in range(parts):
                results[i] = lax.dynamic_update_slice_in_dim(
                    results[i], chunk[i] if apart else chunk, source * concat_size, axis=part_axis
                )
        return results if apart else results[0]

    def to_blocks(head_rows):
        return head_rows.reshape(local_heads, block_count, BLK, DH)

    def head_major(rows):
        return jnp.transpose(rows.reshape(tok_rows, head_count, DH), (1, 0, 2))

    is_last = section_index == last_section
    second = jnp.where(is_last, head_major(cotangent), head_major(inputs[0]))
    stacked = jnp.stack([head_major(queries[0]), second])
    stacked_heads = transpose_seq(stacked, 1, 2)
    query_blocks = to_blocks(stacked_heads[0])
    cot_blocks = to_blocks(stacked_heads[1])
    last_inputs = transpose_seq(head_major(inputs[0]), 0, 1, section=last_section)
    input_heads = jnp.where(is_last, last_inputs, stacked_heads[1])
    values_both = key_pair(to_blocks(input_heads))
    kv_rows = jnp.transpose(key_heads[0].reshape(tok_rows, kv_count, DH), (1, 0, 2))
    if seq_ways == 8 and seq_ways // kv_count == 2:
        parity = seq_index % 2
        fetched = []
        for shift in range(0, seq_ways, 2):
            head = ((seq_index + shift) % seq_ways) // 2
            chunk = lax.dynamic_index_in_dim(kv_rows, head, axis=0, keepdims=False)
            if shift > 0:
                chunk = lax.ppermute(
                    chunk, "seq", [(d, (d + shift) % seq_ways) for d in range(seq_ways)]
                )
            fetched.append(chunk)
        mine = jnp.stack(fetched)
        theirs = lax.ppermute(mine, "seq", [(d, d ^ 1) for d in range(seq_ways)])
        partner = seq_index + 1 - 2 * parity
        blocks = jnp.arange(seq_ways)
        order = jnp.where(
            blocks % 2 == parity,
            ((seq_index - blocks) % seq_ways) // 2,
            seq_ways // 2 + ((partner - blocks) % seq_ways) // 2,
        )
        key_flat = jnp.take(jnp.concatenate([mine, theirs]), order, axis=0).reshape(1, seq_len, DH)
    else:
        kv_pick = (jnp.arange(seq_ways) * local_heads) // group_size
        key_flat = lax.all_to_all(kv_rows[kv_pick], "seq", split_axis=0, concat_axis=1, tiled=True)
    key_blocks = jnp.broadcast_to(
        key_flat.reshape(1, block_count, BLK, DH), (local_heads, block_count, BLK, DH)
    )
    keys_both = key_pair(key_blocks)
    allowed = visible(lengths, block_count, BLK)
    softmax_probs = probabilities(query_blocks, keys_both, allowed, score_scale)
    probs_low = softmax_probs.astype(jnp.bfloat16)

    grad_ins = []
    grad_outs = []
    grad_in = cot_blocks
    for tick in range(section_count):
        sender = last_section - tick
        new_grad = value_grad(probs_low, grad_in, BLK, seq_ways)
        grad_ins.append(grad_in)
        grad_outs.append(new_grad)
        if sender > 0:
            grad_in = lax.ppermute(new_grad, "pipe", [(sender, sender - 1)])

    def by_section(per_tick):
        chosen = per_tick[0]
        for tick in range(1, section_count):
            chosen = jnp.where(section_index == last_section - tick, per_tick[tick], chosen)
        return chosen

    held_in = by_section(grad_ins)
    held_out = by_section(grad_outs)
    grad_query, grad_key = weight_grads(
        softmax_probs,
        probs_low,
        query_blocks,
        keys_both,
        values_both,
        held_in,
        score_scale,
        BLK,
    )
    pair = jnp.transpose(
        jnp.stack([grad_query, held_out]).reshape(2, local_heads, seq_len, DH), (0, 2, 1, 3)
    )
    pair_rows = [
        rows.reshape(tok_rows, full_width) for rows in transpose_seq(pair, 1, 2, apart=True)
    ]
    if local_heads == 1:
        key_part = grad_key.reshape(seq_len, DH)
    else:
        key_part = jnp.sum(grad_key.astype(jnp.float32), axis=0).reshape(seq_len, DH)
    if seq_ways == 8 and seq_ways // kv_count == 2:
        parity = seq_index % 2
        by_parity = key_part.reshape(seq_ways // 2, 2, tok_rows, DH)
        keep = lax.dynamic_index_in_dim(by_parity, parity, axis=1, keepdims=False)
        give = lax.dynamic_index_in_dim(by_parity, 1 - parity, axis=1, keepdims=False)
        got = lax.ppermute(give, "seq", [(d, d ^ 1) for d in range(seq_ways)])
        kept_sum = keep + got
        received = []
        for shift in range(0, seq_ways, 2):
            block = ((seq_index + shift) % seq_ways) // 2
            chunk = lax.dynamic_index_in_dim(kept_sum, block, axis=0, keepdims=False)
            if shift > 0:
                chunk = lax.ppermute(
                    chunk, "seq", [(d, (d + shift) % seq_ways) for d in range(seq_ways)]
                )
            received.append(chunk)
        heads_in = jnp.arange(kv_count)
        order = ((seq_index - 2 * heads_in - parity) % seq_ways) // 2
        key_sum = jnp.transpose(jnp.take(jnp.stack(received), order, axis=0), (1, 0, 2))
    else:
        key_out = lax.all_to_all(
            key_part[:, None, :], "seq", split_axis=0, concat_axis=1, tiled=True
        )
        key_sum = jnp.sum(
            key_out.reshape(tok_rows, kv_count, seq_ways // kv_count, DH).astype(jnp.float32),
            axis=2,
        )
    key_final = key_sum.astype(jnp.bfloat16).reshape(tok_rows, kv_count * DH)
    return (pair_rows[0][None], key_final[None], pair_rows[1][None])


def solution(mesh):
    placed = (
        P("pipe", "seq", None),
        P("pipe", "seq", None),
        P("pipe", "seq", None),
        P("seq", None),
        P(),
    )
    return jax.shard_map(
        on_device,
        mesh=mesh,
        in_specs=placed,
        out_specs=(P("pipe", "seq", None), P("pipe", "seq", None), P("pipe", "seq", None)),
        check_vma=False,
    )
```

```python
import jax
import jax.numpy as jnp
from jax import lax
from jax.sharding import PartitionSpec as P

DH = 128
BLK = 128


def key_pair(block_rows):
    first_block = jnp.broadcast_to(block_rows[:, :1], block_rows.shape)
    return jnp.concatenate([first_block, block_rows], axis=2)


def visible(lengths, block_count, block_len):
    shape = (block_count, block_len, 2 * block_len)
    row_index = lax.broadcasted_iota(jnp.int32, shape, 1)
    col_index = lax.broadcasted_iota(jnp.int32, shape, 2)
    block_index = lax.broadcasted_iota(jnp.int32, shape, 0)
    in_first = col_index < block_len
    offset = jnp.where(in_first, col_index, col_index - block_len)
    own_len = lengths[:, None, None]
    first_ok = in_first & (offset < lengths[0]) & ((block_index > 0) | (offset <= row_index))
    own_ok = (
        jnp.logical_not(in_first) & (block_index > 0) & (offset <= row_index) & (offset < own_len)
    )
    return (first_ok | own_ok)[None]


def fold_keys(key_terms, block_len):
    own_part = key_terms[:, :, block_len:]
    first_part = jnp.sum(key_terms[:, :, :block_len], axis=1)
    return own_part.at[:, 0].add(first_part)


def fold_value(key_terms, block_len, groups):
    own_part = key_terms[:, :, block_len:]
    first_terms = key_terms[:, :, :block_len]
    heads, blocks = first_terms.shape[:2]
    grouped = first_terms.reshape((heads, groups, blocks // groups) + first_terms.shape[2:])
    partial_low = lax.optimization_barrier(jnp.sum(grouped, axis=2).astype(jnp.bfloat16))
    first_part = jnp.sum(partial_low.astype(jnp.float32), axis=1)
    return own_part.at[:, 0].add(first_part)


def probabilities(query_blocks, keys_both, allowed, score_scale):
    scores = (
        jnp.einsum("hbid,hbjd->hbij", query_blocks, keys_both, preferred_element_type=jnp.float32)
        * score_scale
    )
    scores = jnp.where(allowed, scores, -jnp.inf)
    row_max = jnp.max(scores, axis=-1, keepdims=True)
    exp_scores = jnp.exp(scores - row_max)
    return exp_scores / jnp.sum(exp_scores, axis=-1, keepdims=True)


def value_grad(probs_low, grad_blocks, block_len, groups):
    key_terms = jnp.einsum(
        "hbij,hbid->hbjd", probs_low, grad_blocks, preferred_element_type=jnp.float32
    )
    return (grad_blocks.astype(jnp.float32) + fold_value(key_terms, block_len, groups)).astype(
        jnp.bfloat16
    )


def weight_grads(
    softmax_probs, probs_low, query_blocks, keys_both, values_both, grad_blocks, score_scale, block_len
):
    output = jnp.einsum(
        "hbij,hbjd->hbid", probs_low, values_both, preferred_element_type=jnp.float32
    )
    row_dot = jnp.sum(grad_blocks.astype(jnp.float32) * output, axis=-1)[..., None]
    grad_probs = jnp.einsum(
        "hbid,hbjd->hbij", grad_blocks, values_both, preferred_element_type=jnp.float32
    )
    grad_scores = (softmax_probs * (grad_probs - row_dot)).astype(jnp.bfloat16)
    grad_query = (
        jnp.einsum("hbij,hbjd->hbid", grad_scores, keys_both, preferred_element_type=jnp.float32)
        * score_scale
    ).astype(jnp.bfloat16)
    key_terms = jnp.einsum(
        "hbij,hbid->hbjd", grad_scores, query_blocks, preferred_element_type=jnp.float32
    )
    grad_key = (fold_keys(key_terms, block_len) * score_scale).astype(jnp.bfloat16)
    return (grad_query, grad_key)


def on_device(queries, key_heads, inputs, cotangent, lengths):
    section_count = lax.axis_size("pipe")
    section_index = lax.axis_index("pipe")
    seq_ways = lax.axis_size("seq")
    tok_rows = queries.shape[1]
    full_width = queries.shape[2]
    head_count = full_width // DH
    kv_count = key_heads.shape[2] // DH
    group_size = head_count // kv_count
    seq_len = tok_rows * seq_ways
    block_count = seq_len // BLK
    local_heads = head_count // seq_ways
    score_scale = DH ** (-0.5)
    last_section = section_count - 1

    seq_index = lax.axis_index("seq")

    def transpose_seq(value, split_axis, concat_axis, section=None):
        if seq_ways > 8:
            return lax.all_to_all(value, "seq", split_axis, concat_axis, tiled=True)
        split_size = value.shape[split_axis] // seq_ways
        concat_size = value.shape[concat_axis]
        out_shape = list(value.shape)
        out_shape[split_axis] = split_size
        out_shape[concat_axis] = concat_size * seq_ways
        result = jnp.zeros(out_shape, value.dtype)
        for shift in range(seq_ways):
            target = (seq_index + shift) % seq_ways
            chunk = lax.dynamic_slice_in_dim(value, target * split_size, split_size, axis=split_axis)
            if shift > 0 and section is None:
                chunk = lax.ppermute(
                    chunk, "seq", [(s, (s + shift) % seq_ways) for s in range(seq_ways)]
                )
            elif shift > 0:
                base = section * seq_ways
                chunk = lax.ppermute(
                    chunk,
                    ("pipe", "seq"),
                    [(base + s, base + (s + shift) % seq_ways) for s in range(seq_ways)],
                )
            source = (seq_index + seq_ways - shift) % seq_ways
            result = lax.dynamic_update_slice_in_dim(
                result, chunk, source * concat_size, axis=concat_axis
            )
        return result

    def to_blocks(head_rows):
        return head_rows.reshape(local_heads, block_count, BLK, DH)

    def head_major(rows):
        return jnp.transpose(rows.reshape(tok_rows, head_count, DH), (1, 0, 2))

    is_last = section_index == last_section
    second = jnp.where(is_last, head_major(cotangent), head_major(inputs[0]))
    stacked = jnp.stack([head_major(queries[0]), second])
    stacked_heads = transpose_seq(stacked, 1, 2)
    query_blocks = to_blocks(stacked_heads[0])
    cot_blocks = to_blocks(stacked_heads[1])
    last_inputs = transpose_seq(head_major(inputs[0]), 0, 1, section=last_section)
    input_heads = jnp.where(is_last, last_inputs, stacked_heads[1])
    values_both = key_pair(to_blocks(input_heads))
    kv_rows = jnp.transpose(key_heads[0].reshape(tok_rows, kv_count, DH), (1, 0, 2))
    if seq_ways == 8 and seq_ways // kv_count == 2:
        parity = seq_index % 2
        fetched = []
        for shift in range(0, seq_ways, 2):
            head = ((seq_index + shift) % seq_ways) // 2
            chunk = lax.dynamic_index_in_dim(kv_rows, head, axis=0, keepdims=False)
            if shift > 0:
                chunk = lax.ppermute(
                    chunk, "seq", [(d, (d + shift) % seq_ways) for d in range(seq_ways)]
                )
            fetched.append(chunk)
        mine = jnp.stack(fetched)
        theirs = lax.ppermute(mine, "seq", [(d, d ^ 1) for d in range(seq_ways)])
        partner = seq_index + 1 - 2 * parity
        blocks = jnp.arange(seq_ways)
        order = jnp.where(
            blocks % 2 == parity,
            ((seq_index - blocks) % seq_ways) // 2,
            seq_ways // 2 + ((partner - blocks) % seq_ways) // 2,
        )
        key_flat = jnp.take(jnp.concatenate([mine, theirs]), order, axis=0).reshape(1, seq_len, DH)
    else:
        kv_pick = (jnp.arange(seq_ways) * local_heads) // group_size
        key_flat = lax.all_to_all(kv_rows[kv_pick], "seq", split_axis=0, concat_axis=1, tiled=True)
    key_blocks = jnp.broadcast_to(
        key_flat.reshape(1, block_count, BLK, DH), (local_heads, block_count, BLK, DH)
    )
    keys_both = key_pair(key_blocks)
    allowed = visible(lengths, block_count, BLK)
    softmax_probs = probabilities(query_blocks, keys_both, allowed, score_scale)
    probs_low = softmax_probs.astype(jnp.bfloat16)

    grad_ins = []
    grad_outs = []
    grad_in = cot_blocks
    for tick in range(section_count):
        sender = last_section - tick
        new_grad = value_grad(probs_low, grad_in, BLK, seq_ways)
        grad_ins.append(grad_in)
        grad_outs.append(new_grad)
        if sender > 0:
            grad_in = lax.ppermute(new_grad, "pipe", [(sender, sender - 1)])

    def by_section(per_tick):
        chosen = per_tick[0]
        for tick in range(1, section_count):
            chosen = jnp.where(section_index == last_section - tick, per_tick[tick], chosen)
        return chosen

    held_in = by_section(grad_ins)
    held_out = by_section(grad_outs)
    grad_query, grad_key = weight_grads(
        softmax_probs,
        probs_low,
        query_blocks,
        keys_both,
        values_both,
        held_in,
        score_scale,
        BLK,
    )
    pair = jnp.transpose(
        jnp.stack([grad_query, held_out]).reshape(2, local_heads, seq_len, DH), (0, 2, 1, 3)
    )
    pair_out = transpose_seq(pair, 1, 2)
    pair_rows = pair_out.reshape(2, tok_rows, full_width)
    if local_heads == 1:
        key_part = grad_key.reshape(seq_len, DH)
    else:
        key_part = jnp.sum(grad_key.astype(jnp.float32), axis=0).reshape(seq_len, DH)
    if seq_ways == 8 and seq_ways // kv_count == 2:
        parity = seq_index % 2
        by_parity = key_part.reshape(seq_ways // 2, 2, tok_rows, DH)
        keep = lax.dynamic_index_in_dim(by_parity, parity, axis=1, keepdims=False)
        give = lax.dynamic_index_in_dim(by_parity, 1 - parity, axis=1, keepdims=False)
        got = lax.ppermute(give, "seq", [(d, d ^ 1) for d in range(seq_ways)])
        kept_sum = keep + got
        received = []
        for shift in range(0, seq_ways, 2):
            block = ((seq_index + shift) % seq_ways) // 2
            chunk = lax.dynamic_index_in_dim(kept_sum, block, axis=0, keepdims=False)
            if shift > 0:
                chunk = lax.ppermute(
                    chunk, "seq", [(d, (d + shift) % seq_ways) for d in range(seq_ways)]
                )
            received.append(chunk)
        heads_in = jnp.arange(kv_count)
        order = ((seq_index - 2 * heads_in - parity) % seq_ways) // 2
        key_sum = jnp.take(jnp.stack(received, axis=1), order, axis=1)
    else:
        key_out = lax.all_to_all(
            key_part[:, None, :], "seq", split_axis=0, concat_axis=1, tiled=True
        )
        key_sum = jnp.sum(
            key_out.reshape(tok_rows, kv_count, seq_ways // kv_count, DH).astype(jnp.float32),
            axis=2,
        )
    key_final = key_sum.astype(jnp.bfloat16).reshape(tok_rows, kv_count * DH)
    return (pair_rows[0][None], key_final[None], pair_rows[1][None])


def solution(mesh):
    placed = (
        P("pipe", "seq", None),
        P("pipe", "seq", None),
        P("pipe", "seq", None),
        P("seq", None),
        P(),
    )
    return jax.shard_map(
        on_device,
        mesh=mesh,
        in_specs=placed,
        out_specs=(P("pipe", "seq", None), P("pipe", "seq", None), P("pipe", "seq", None)),
        check_vma=False,
    )
```
